32 devices in a mesh: ens: 4 (over x, core), lat: 2 (over y), lon: 4 (over z).
Axes of the slice: x: 2, y: 2, z: 4, core: 2. Of those that a mesh axis runs over, the one named last changes fastest.
Arguments:
- state_field: bfloat16 [4, 256, 4, 512], P('ens', None, 'lat', 'lon'), may hold values from -6 to 6
- first_weight: bfloat16 [3, 256, 256], replicated, may hold values from -0.21875 to 0.21875
- second_weight: bfloat16 [3, 256, 256], replicated, may hold values from -0.21875 to 0.21875
- quadrature: float32 [4, 3, 12], P('lat'), may hold values from 0.05 to 0.4
- lat_offsets: int32 [4, 3, 12], P('lat'), may hold values from -1 to 1, as said below
- lon_offsets: int32 [4, 3, 12], P('lat'), may hold values from -4 to 4, as said below
- cotangent: bfloat16 [4, 256, 4, 512], P('ens', None, 'lat', 'lon'), may hold values from -6 to 6
Outputs:
- layer_output: bfloat16 [4, 256, 4, 512], P('ens', None, 'lat', 'lon')
- state_grad: bfloat16 [4, 256, 4, 512], P('ens', None, 'lat', 'lon')
- first_grad: float32 [3, 256, 256], replicated
- second_grad: float32 [3, 256, 256], replicated
The draws below stay inside these ranges and needn't reach their ends.
Inputs may be any that keep to these rules, and one draw needn't show every extreme that they name: `lat_offsets`: for every row and basis function the first three support points have latitude offsets 0, -1 and 1. `lon_offsets`: in a row p rows from the nearer pole the longitude offsets lie within plus or minus max(2, 4 - p), and the first three support points have offsets 0, minus that bound and that bound.
All inputs are finite; a program needn't handle non-finite values.
Results may differ from the reference program's by a relative error of at most 0.013.
Values may be sent and summed in bfloat16 or wider, within the bound.
No kernel may reach another device: no remote copies, remote signals or barrier semaphores. Data moves between devices by JAX's collectives and lax.ppermute only.
A program may use at most 64 MiB of HBM per device.

```python
import math
from functools import partial
import jax
import jax.numpy as jnp
from jax import lax

CHANNELS = 256
BASIS = 3
SUPPORT = 12
LAT_REACH = 1
LON_REACH = 4
MEMBERS = 4
NLAT = 4
NLON = 512


def draw_lat_offsets(key, part):
    sub_key = jax.random.fold_in(key, 11)
    table_shape = (NLAT, BASIS, SUPPORT)
    values = jax.random.randint(sub_key, table_shape, -LAT_REACH, LAT_REACH + 1)
    slot_index = lax.broadcasted_iota(jnp.int32, table_shape, 2)
    values = jnp.where(slot_index == 0, 0, values)
    values = jnp.where(slot_index == 1, -LAT_REACH, values)
    values = jnp.where(slot_index == 2, LAT_REACH, values)
    return values.astype(jnp.int32)


def draw_lon_offsets(key, part):
    sub_key = jax.random.fold_in(key, 23)
    table_shape = (NLAT, BASIS, SUPPORT)
    row_index = lax.broadcasted_iota(jnp.int32, table_shape, 0)
    pole_distance = jnp.minimum(row_index, NLAT - 1 - row_index)
    reach_row = jnp.maximum(2, LON_REACH - pole_distance)
    raw_values = jax.random.randint(sub_key, table_shape, 0, 65536)
    values = raw_values % (2 * reach_row + 1) - reach_row
    slot_index = lax.broadcasted_iota(jnp.int32, table_shape, 2)
    values = jnp.where(slot_index == 0, 0, values)
    values = jnp.where(slot_index == 1, -reach_row, values)
    values = jnp.where(slot_index == 2, reach_row, values)
    return values.astype(jnp.int32)


def level_of(rng, extent, shards, least, largest):
    gain = 1.0
    for position, shards_of in shards:
        steps = jax.random.uniform(jax.random.fold_in(jax.random.fold_in(rng, 6), position), (shards_of,), jnp.float32, least / len(shards), largest / len(shards))
        gain = gain * jnp.repeat(jnp.exp(steps), extent[position] // shards_of).reshape((-1,) + (1,) * (len(extent) - 1 - position))
    return gain


def gaussian(stream_key, extent, scale, most, pieces=(), kind=jnp.bfloat16):
    values = scale * jax.random.normal(stream_key, extent, jnp.float32)
    if pieces:
        values = values * level_of(stream_key, extent, pieces, -0.22, 0.18)
    return jnp.clip(values, -most, most).astype(kind)


def setup_inputs(seed: int = 0) -> dict:
    seeds = jax.random.split(jax.random.key(seed), 8)
    state_field = gaussian(seeds[0], (MEMBERS, CHANNELS, NLAT, NLON), 1.0, 6.0, ((0, 4), (2, 2), (3, 4)))
    first_weight = gaussian(seeds[1], (BASIS, CHANNELS, CHANNELS), (CHANNELS * BASIS) ** -0.5, 0.21875)
    second_weight = gaussian(seeds[2], (BASIS, CHANNELS, CHANNELS), (CHANNELS * BASIS) ** -0.5, 0.21875)
    quadrature = jnp.clip(jnp.exp(math.log(0.4) - 2.0794415 * jax.random.uniform(seeds[3], (NLAT, BASIS, SUPPORT), jnp.float32) ** level_of(seeds[3], (NLAT, BASIS, SUPPORT), ((0, 2),), -0.2, 0.2)), 0.05, 0.4)
    lat_offsets = draw_lat_offsets(jax.random.fold_in(seeds[7], 71), 0)
    lon_offsets = draw_lon_offsets(jax.random.fold_in(seeds[7], 71), 0)
    cotangent = gaussian(seeds[6], (MEMBERS, CHANNELS, NLAT, NLON), 1.0, 6.0, ((0, 4), (2, 2), (3, 4)))
    return dict(state_field=state_field, first_weight=first_weight, second_weight=second_weight, quadrature=quadrature, lat_offsets=lat_offsets, lon_offsets=lon_offsets, cotangent=cotangent)


def coefficients(quadrature, lat_offsets, lon_offsets):
    lat_levels = jnp.arange(2 * LAT_REACH + 1, dtype=jnp.int32)
    lon_levels = jnp.arange(2 * LON_REACH + 1, dtype=jnp.int32)
    lat_onehot = (lat_offsets[..., None] + LAT_REACH == lat_levels).astype(jnp.float32)
    lon_onehot = (lon_offsets[..., None] + LON_REACH == lon_levels).astype(jnp.float32)
    stencil = jnp.einsum('rks,rksa,rksd->krad', quadrature, lat_onehot, lon_onehot, precision=lax.Precision.HIGHEST)
    return stencil.astype(jnp.bfloat16)

def spread(source, stencil):
    lat_taps = 2 * LAT_REACH + 1
    padded = jnp.pad(source, ((0, 0), (LAT_REACH, LAT_REACH), (0, 0)))

    def one_row(row_index):
        nearby = lax.dynamic_slice_in_dim(padded, row_index, lat_taps, 1)
        shifted = jnp.stack([jnp.roll(nearby, LON_REACH - offset, axis=2) for offset in range(2 * LON_REACH + 1)], axis=2)
        weights = lax.dynamic_index_in_dim(stencil, row_index, 1, keepdims=False)
        return jnp.einsum('cadj,kad->ckj', shifted, weights, precision=lax.Precision.HIGHEST)
    rows_out = lax.map(one_row, jnp.arange(NLAT, dtype=jnp.int32))
    return jnp.transpose(rows_out, (1, 2, 0, 3))

def mix_channels(weight, spreaded):
    return jnp.einsum('koc,ckij->oij', weight.astype(jnp.float32), spreaded.astype(jnp.float32), precision=lax.Precision.HIGHEST)

def unmix(weight, gradient):
    return jnp.einsum('koc,oij->ckij', weight.astype(jnp.float32), gradient.astype(jnp.float32), precision=lax.Precision.HIGHEST).astype(jnp.bfloat16)

def filter_term(gradient, spreaded):
    return jnp.einsum('oij,ckij->koc', gradient.astype(jnp.float32), spreaded.astype(jnp.float32), precision=lax.Precision.HIGHEST)

def reference(state_field, first_weight, second_weight, quadrature, lat_offsets, lon_offsets, cotangent):
    stencil = coefficients(quadrature, lat_offsets, lon_offsets).astype(jnp.float32)
    outputs = []
    state_grads = []
    first_sum = jnp.zeros((BASIS, CHANNELS, CHANNELS), jnp.float32)
    second_sum = jnp.zeros((BASIS, CHANNELS, CHANNELS), jnp.float32)
    for member in range(MEMBERS):
        source = state_field[member].astype(jnp.float32)
        first_spread = spread(source, stencil).astype(jnp.bfloat16)
        hidden = mix_channels(first_weight, first_spread)
        activation = jax.nn.gelu(hidden).astype(jnp.bfloat16)
        back_second = jax.vjp(partial(spread, stencil=stencil), activation.astype(jnp.float32))[1]
        second_spread = spread(activation.astype(jnp.float32), stencil).astype(jnp.bfloat16)
        outputs.append(mix_channels(second_weight, second_spread).astype(jnp.bfloat16))
        gradient = cotangent[member]
        second_sum = second_sum + filter_term(gradient, second_spread)
        second_mixed = unmix(second_weight, gradient)
        activation_grad = back_second(second_mixed.astype(jnp.float32))[0].astype(jnp.bfloat16)
        hidden_grad = jax.vjp(jax.nn.gelu, hidden)[1](activation_grad.astype(jnp.float32))[0].astype(jnp.bfloat16)
        first_sum = first_sum + filter_term(hidden_grad, first_spread)
        first_mixed = unmix(first_weight, hidden_grad)
        back_first = jax.vjp(partial(spread, stencil=stencil), source)[1]
        state_grads.append(back_first(first_mixed.astype(jnp.float32))[0].astype(jnp.bfloat16))
    grad_scale = 1.0 / math.sqrt(MEMBERS * NLAT * NLON)
    return (jnp.stack(outputs), jnp.stack(state_grads), first_sum * grad_scale, second_sum * grad_scale)
```

```python
import math

import jax
import jax.numpy as jnp
from jax import lax
from jax.sharding import PartitionSpec as P

LAT_REACH = 1
LON_REACH = 4


def with_halo(block, sides, width, periodic):
    for axis, dim in sides:
        count = lax.axis_size(axis)
        forward = [(i, i + 1) for i in range(count - 1)]
        if periodic:
            forward.append((count - 1, 0))
        backward = [(target, source) for source, target in forward]
        low = lax.ppermute(
            lax.slice_in_dim(block, block.shape[dim] - width, None, axis=dim), axis, forward
        )
        high = lax.ppermute(lax.slice_in_dim(block, 0, width, axis=dim), axis, backward)
        block = jnp.concatenate([low, block, high], axis=dim)
    return block


def passed_along(value, axis, by):
    devices = lax.axis_size(axis)
    return lax.ppermute(value, axis, [(i, (i + by) % devices) for i in range(devices)])


def passed_along_2(value, axis, steps):
    count = lax.axis_size(axis)
    leading, last = (max(0, -steps), min(count, count - steps))
    return lax.ppermute(value, axis, [(source, source + steps) for source in range(leading, last)])


def halving_sum(value, axes):
    stages = []
    for axis in axes:
        bit = 1
        while bit < lax.axis_size(axis):
            stages.append((axis, bit))
            bit *= 2
    flat = value.reshape(-1)
    for axis, bit in stages:
        pairs = [(i, i ^ bit) for i in range(lax.axis_size(axis))]
        upper = (lax.axis_index(axis) // bit) % 2
        half = flat.shape[0] // 2
        keep = lax.dynamic_slice_in_dim(flat, upper * half, half)
        send = lax.dynamic_slice_in_dim(flat, (1 - upper) * half, half)
        flat = keep + lax.ppermute(send, axis, pairs)
    for axis, bit in reversed(stages):
        pairs = [(i, i ^ bit) for i in range(lax.axis_size(axis))]
        upper = (lax.axis_index(axis) // bit) % 2
        other = lax.ppermute(flat, axis, pairs)
        flat = jnp.where(
            upper == 1, jnp.concatenate([other, flat]), jnp.concatenate([flat, other])
        )
    return flat.reshape(value.shape)


def coefficients(quadrature, lat_offsets, lon_offsets):
    lat_levels = jnp.arange(2 * LAT_REACH + 1, dtype=jnp.int32)
    lon_levels = jnp.arange(2 * LON_REACH + 1, dtype=jnp.int32)
    lat_onehot = (lat_offsets[..., None] + LAT_REACH == lat_levels).astype(jnp.float32)
    lon_onehot = (lon_offsets[..., None] + LON_REACH == lon_levels).astype(jnp.float32)
    stencil = jnp.einsum(
        "rks,rksa,rksd->krad", quadrature, lat_onehot, lon_onehot, precision=lax.Precision.HIGHEST
    )
    return stencil.astype(jnp.bfloat16)


def lon_picker(col_count):
    span_count = 2 * LON_REACH + 1
    wide_count = col_count + 2 * LON_REACH
    table_shape = (span_count, wide_count, col_count)
    offset_level = lax.broadcasted_iota(jnp.int32, table_shape, 0)
    source = lax.broadcasted_iota(jnp.int32, table_shape, 1)
    target = lax.broadcasted_iota(jnp.int32, table_shape, 2)
    matches = source - target == offset_level
    return matches.astype(jnp.bfloat16)


def widen(values):
    wide_lon = with_halo(values, (("lon", 2),), LON_REACH, True)
    return with_halo(wide_lon, (("lat", 1),), LAT_REACH, False)


def lon_pass(piece, steps):
    return passed_along(piece, "lon", steps)


def lat_pass(piece, steps):
    return passed_along_2(piece.astype(jnp.bfloat16), "lat", steps).astype(piece.dtype)


def mix_channels(weight, spreaded):
    return jnp.einsum("koc,cikj->oij", weight, spreaded, preferred_element_type=jnp.float32)


def filter_term(gradient, spreaded):
    return jnp.einsum("oij,cikj->koc", gradient, spreaded, preferred_element_type=jnp.float32)


def body(state_field, first_weight, second_weight, quadrature, lat_offsets, lon_offsets, cotangent):
    source = state_field[0]
    channels, row_count, col_count = source.shape
    lat_taps = 2 * LAT_REACH + 1
    wide_count = col_count + 2 * LON_REACH
    stencil = coefficients(quadrature, lat_offsets, lon_offsets)
    basis_count = stencil.shape[0]
    forward_band = jnp.einsum(
        "kiad,dpq->iapkq", stencil, lon_picker(col_count), preferred_element_type=jnp.float32
    )
    forward_band = forward_band.astype(jnp.bfloat16).reshape(
        row_count, lat_taps * wide_count, basis_count * col_count
    )

    def spread(values):
        extended = widen(values)
        stacked = jnp.stack(
            [extended[:, offset : offset + row_count] for offset in range(lat_taps)], axis=2
        )
        stacked = stacked.reshape(channels, row_count, lat_taps * wide_count)
        mixed = jnp.einsum(
            "cin,inm->cim", stacked, forward_band, preferred_element_type=jnp.float32
        )
        return mixed.reshape(channels, row_count, basis_count, col_count).astype(jnp.bfloat16)

    first_spread = spread(source)
    hidden = mix_channels(first_weight, first_spread)
    activation = jax.nn.gelu(hidden).astype(jnp.bfloat16)
    second_spread = spread(activation)
    layer_output = mix_channels(second_weight, second_spread).astype(jnp.bfloat16)
    gradient = cotangent[0]
    second_sum = filter_term(gradient, second_spread)

    def carry_back(weight, grad_rows):
        mixed_grad = jnp.einsum(
            "koc,oij->cikj", weight, grad_rows, preferred_element_type=jnp.float32
        ).astype(jnp.bfloat16)
        partial_rows = jnp.einsum(
            "cim,inm->cin",
            mixed_grad.reshape(channels, row_count, basis_count * col_count),
            forward_band,
            preferred_element_type=jnp.float32,
        )
        partial_rows = partial_rows.reshape(channels, row_count, lat_taps, wide_count)
        extended = jnp.zeros((channels, row_count + 2 * LAT_REACH, wide_count), jnp.float32)
        for offset in range(lat_taps):
            extended = extended + jnp.pad(
                partial_rows[:, :, offset], ((0, 0), (offset, lat_taps - 1 - offset), (0, 0))
            )
        left_rim = extended[:, :, :LON_REACH]
        right_rim = extended[:, :, LON_REACH + col_count :]
        core_block = extended[:, :, LON_REACH : LON_REACH + col_count]
        core_block = (
            core_block
            + jnp.pad(lon_pass(left_rim, -1), ((0, 0), (0, 0), (col_count - LON_REACH, 0)))
            + jnp.pad(lon_pass(right_rim, 1), ((0, 0), (0, 0), (0, col_count - LON_REACH)))
        )
        top_rows = core_block[:, :LAT_REACH]
        bottom_rows = core_block[:, LAT_REACH + row_count :]
        inner_rows = core_block[:, LAT_REACH : LAT_REACH + row_count]
        inner_rows = (
            inner_rows
            + jnp.pad(lat_pass(top_rows, -1), ((0, 0), (row_count - LAT_REACH, 0), (0, 0)))
            + jnp.pad(lat_pass(bottom_rows, 1), ((0, 0), (0, row_count - LAT_REACH), (0, 0)))
        )
        return inner_rows.astype(jnp.bfloat16)

    activation_grad = carry_back(second_weight, gradient)
    hidden_grad = jax.vjp(jax.nn.gelu, hidden)[1](activation_grad.astype(jnp.float32))[0].astype(
        jnp.bfloat16
    )
    first_sum = filter_term(hidden_grad, first_spread)
    state_grad = carry_back(first_weight, hidden_grad)
    first_sum, second_sum = jnp.split(
        halving_sum(jnp.concatenate([first_sum, second_sum]), ("ens", "lat", "lon")), 2
    )
    member_total = state_field.shape[0] * lax.axis_size("ens")
    grad_scale = 1.0 / math.sqrt(
        member_total * row_count * lax.axis_size("lat") * col_count * lax.axis_size("lon")
    )
    return (layer_output[None], state_grad[None], first_sum * grad_scale, second_sum * grad_scale)


def solution(mesh):
    in_specs = (
        P("ens", None, "lat", "lon"),
        P(),
        P(),
        P("lat", None, None),
        P("lat", None, None),
        P("lat", None, None),
        P("ens", None, "lat", "lon"),
    )
    out_specs = (P("ens", None, "lat", "lon"), P("ens", None, "lat", "lon"), P(), P())
    return jax.shard_map(body, mesh=mesh, in_specs=in_specs, out_specs=out_specs, check_vma=False)
```

```python
import math

import jax
import jax.numpy as jnp
from jax import lax
from jax.sharding import PartitionSpec as P

LAT_REACH = 1
LON_REACH = 4
LAT_HALO = 2 * LAT_REACH
LON_HALO = 2 * LON_REACH


def halving_sum(value, axes):
    stages = []
    for axis in axes:
        bit = 1
        while bit < lax.axis_size(axis):
            stages.append((axis, bit))
            bit *= 2
    flat = value.reshape(-1)
    for axis, bit in stages:
        pairs = [(i, i ^ bit) for i in range(lax.axis_size(axis))]
        upper = (lax.axis_index(axis) // bit) % 2
        half = flat.shape[0] // 2
        keep = lax.dynamic_slice_in_dim(flat, upper * half, half)
        send = lax.dynamic_slice_in_dim(flat, (1 - upper) * half, half)
        flat = keep + lax.ppermute(send, axis, pairs)
    for axis, bit in reversed(stages):
        pairs = [(i, i ^ bit) for i in range(lax.axis_size(axis))]
        upper = (lax.axis_index(axis) // bit) % 2
        other = lax.ppermute(flat, axis, pairs)
        flat = jnp.where(
            upper == 1, jnp.concatenate([other, flat]), jnp.concatenate([flat, other])
        )
    return flat.reshape(value.shape)


def lat_halo(block, dim, width):
    count = lax.axis_size("lat")
    rows = block.shape[dim]
    above = lax.ppermute(
        lax.slice_in_dim(block, rows - width, rows, axis=dim),
        "lat",
        [(i, i + 1) for i in range(count - 1)],
    )
    below = lax.ppermute(
        lax.slice_in_dim(block, 0, width, axis=dim), "lat", [(i + 1, i) for i in range(count - 1)]
    )
    return jnp.concatenate([above, block, below], axis=dim)


def lon_halo(block, width):
    count = lax.axis_size("lon")
    cols = block.shape[-1]
    left = lax.ppermute(block[..., cols - width :], "lon", [(i, (i + 1) % count) for i in range(count)])
    right = lax.ppermute(block[..., :width], "lon", [(i, (i - 1) % count) for i in range(count)])
    return jnp.concatenate([left, block, right], axis=-1)


def coefficients(quadrature, lat_offsets, lon_offsets):
    lat_levels = jnp.arange(2 * LAT_REACH + 1, dtype=jnp.int32)
    lon_levels = jnp.arange(2 * LON_REACH + 1, dtype=jnp.int32)
    lat_onehot = (lat_offsets[..., None] + LAT_REACH == lat_levels).astype(jnp.float32)
    lon_onehot = (lon_offsets[..., None] + LON_REACH == lon_levels).astype(jnp.float32)
    stencil = jnp.einsum(
        "rks,rksa,rksd->krad", quadrature, lat_onehot, lon_onehot, precision=lax.Precision.HIGHEST
    )
    return stencil.astype(jnp.bfloat16)


def lon_picker(col_count):
    span_count = 2 * LON_REACH + 1
    wide_count = col_count + 2 * LON_REACH
    table_shape = (span_count, wide_count, col_count)
    offset_level = lax.broadcasted_iota(jnp.int32, table_shape, 0)
    source = lax.broadcasted_iota(jnp.int32, table_shape, 1)
    target = lax.broadcasted_iota(jnp.int32, table_shape, 2)
    matches = source - target == offset_level
    return matches.astype(jnp.bfloat16)


def band_of(stencil, col_count):
    row_count = stencil.shape[1]
    basis_count = stencil.shape[0]
    lat_taps = 2 * LAT_REACH + 1
    band = jnp.einsum(
        "kiad,dpq->iapkq", stencil, lon_picker(col_count), preferred_element_type=jnp.float32
    )
    return band.astype(jnp.bfloat16).reshape(
        row_count, lat_taps * (col_count + 2 * LON_REACH), basis_count * col_count
    )


def spread(values, band, basis_count):
    channels = values.shape[0]
    row_count = values.shape[1] - 2 * LAT_REACH
    col_count = values.shape[2] - 2 * LON_REACH
    lat_taps = 2 * LAT_REACH + 1
    stacked = jnp.stack(
        [values[:, offset : offset + row_count] for offset in range(lat_taps)], axis=2
    )
    stacked = stacked.reshape(channels, row_count, lat_taps * values.shape[2])
    mixed = jnp.einsum("cin,inm->cim", stacked, band, preferred_element_type=jnp.float32)
    return mixed.reshape(channels, row_count, basis_count, col_count)


def spread_adjoint(mixed, band):
    channels, row_count, basis_count, col_count = mixed.shape
    lat_taps = 2 * LAT_REACH + 1
    partial = jnp.einsum(
        "cim,inm->cin",
        mixed.reshape(channels, row_count, basis_count * col_count),
        band,
        preferred_element_type=jnp.float32,
    )
    partial = partial.reshape(channels, row_count, lat_taps, col_count + 2 * LON_REACH)
    partial = partial[:, :, :, LON_HALO : col_count]
    out_rows = row_count - LAT_HALO
    total = partial[:, LAT_HALO : LAT_HALO + out_rows, 0]
    for offset in range(1, lat_taps):
        start = LAT_HALO - offset
        total = total + partial[:, start : start + out_rows, offset]
    return total


def mix_channels(weight, spreaded):
    return jnp.einsum("koc,cikj->oij", weight, spreaded, preferred_element_type=jnp.float32)


def unmix(weight, grad_rows):
    return jnp.einsum(
        "koc,oij->cikj", weight, grad_rows, preferred_element_type=jnp.float32
    ).astype(jnp.bfloat16)


def filter_term(gradient, spreaded):
    return jnp.einsum("oij,cikj->koc", gradient, spreaded, preferred_element_type=jnp.float32)


def body(state_field, first_weight, second_weight, quadrature, lat_offsets, lon_offsets, cotangent):
    source = state_field[0]
    gradient = cotangent[0]
    channels, row_count, col_count = source.shape
    stencil = coefficients(quadrature, lat_offsets, lon_offsets)
    basis_count = stencil.shape[0]

    packed = jnp.concatenate([source, gradient], axis=0)
    framed = lat_halo(lon_halo(packed, LON_HALO), 1, LAT_HALO)
    source_wide, gradient_wide = framed[:channels], framed[channels:]
    stencil_wide = lat_halo(stencil, 1, LAT_HALO)

    total_rows = row_count * lax.axis_size("lat")
    first_row = lax.axis_index("lat") * row_count
    near_rows = first_row - LAT_REACH + jnp.arange(row_count + 2 * LAT_REACH)
    near_valid = ((near_rows >= 0) & (near_rows < total_rows))[None, :, None]

    near_band = band_of(stencil_wide[:, LAT_REACH : LAT_REACH + row_count + 2 * LAT_REACH], col_count + LON_HALO)
    own_band = band_of(stencil, col_count)
    wide_band = band_of(stencil_wide, col_count + 2 * LON_HALO)

    first_near = spread(source_wide, near_band, basis_count).astype(jnp.bfloat16)
    hidden = mix_channels(first_weight, first_near)
    activation = jnp.where(near_valid, jax.nn.gelu(hidden), 0.0).astype(jnp.bfloat16)
    second_spread = spread(activation, own_band, basis_count).astype(jnp.bfloat16)
    layer_output = mix_channels(second_weight, second_spread).astype(jnp.bfloat16)
    own_gradient = gradient_wide[:, LAT_HALO : LAT_HALO + row_count, LON_HALO : LON_HALO + col_count]
    second_sum = filter_term(own_gradient, second_spread)

    second_mixed = unmix(second_weight, gradient_wide)
    activation_grad = spread_adjoint(second_mixed, wide_band).astype(jnp.bfloat16)
    hidden_grad = jax.vjp(jax.nn.gelu, hidden)[1](activation_grad.astype(jnp.float32))[0]
    hidden_grad = jnp.where(near_valid, hidden_grad, 0.0).astype(jnp.bfloat16)
    own_hidden_grad = hidden_grad[:, LAT_REACH : LAT_REACH + row_count, LON_REACH : LON_REACH + col_count]
    own_first = first_near[:, LAT_REACH : LAT_REACH + row_count, :, LON_REACH : LON_REACH + col_count]
    first_sum = filter_term(own_hidden_grad, own_first)
    first_mixed = unmix(first_weight, hidden_grad)
    state_grad = spread_adjoint(first_mixed, near_band).astype(jnp.bfloat16)

    first_sum, second_sum = jnp.split(
        halving_sum(jnp.concatenate([first_sum, second_sum]), ("ens", "lat", "lon")), 2
    )
    member_total = state_field.shape[0] * lax.axis_size("ens")
    grad_scale = 1.0 / math.sqrt(
        member_total * row_count * lax.axis_size("lat") * col_count * lax.axis_size("lon")
    )
    return (layer_output[None], state_grad[None], first_sum * grad_scale, second_sum * grad_scale)


def solution(mesh):
    in_specs = (
        P("ens", None, "lat", "lon"),
        P(),
        P(),
        P("lat", None, None),
        P("lat", None, None),
        P("lat", None, None),
        P("ens", None, "lat", "lon"),
    )
    out_specs = (P("ens", None, "lat", "lon"), P("ens", None, "lat", "lon"), P(), P())
    return jax.shard_map(body, mesh=mesh, in_specs=in_specs, out_specs=out_specs, check_vma=False)
```

```python
import math

import jax
import jax.numpy as jnp
from jax import lax
from jax.sharding import PartitionSpec as P

LAT_REACH = 1
LON_REACH = 4
LAT_HALO = 2 * LAT_REACH
LON_HALO = 2 * LON_REACH


def halving_sum(value, axes):
    stages = []
    for axis in axes:
        bit = 1
        while bit < lax.axis_size(axis):
            stages.append((axis, bit))
            bit *= 2
    flat = value.reshape(-1)
    for axis, bit in stages:
        pairs = [(i, i ^ bit) for i in range(lax.axis_size(axis))]
        upper = (lax.axis_index(axis) // bit) % 2
        half = flat.shape[0] // 2
        keep = lax.dynamic_slice_in_dim(flat, upper * half, half)
        send = lax.dynamic_slice_in_dim(flat, (1 - upper) * half, half)
        flat = keep + lax.ppermute(send, axis, pairs)
    for axis, bit in reversed(stages):
        pairs = [(i, i ^ bit) for i in range(lax.axis_size(axis))]
        upper = (lax.axis_index(axis) // bit) % 2
        other = lax.ppermute(flat, axis, pairs)
        flat = jnp.where(
            upper == 1, jnp.concatenate([other, flat]), jnp.concatenate([flat, other])
        )
    return flat.reshape(value.shape)


def lat_halo(block, dim, width):
    count = lax.axis_size("lat")
    rows = block.shape[dim]
    above = lax.ppermute(
        lax.slice_in_dim(block, rows - width, rows, axis=dim),
        "lat",
        [(i, i + 1) for i in range(count - 1)],
    )
    below = lax.ppermute(
        lax.slice_in_dim(block, 0, width, axis=dim), "lat", [(i + 1, i) for i in range(count - 1)]
    )
    return jnp.concatenate([above, block, below], axis=dim)


def lon_halo(block, width):
    count = lax.axis_size("lon")
    cols = block.shape[-1]
    left = lax.ppermute(block[..., cols - width :], "lon", [(i, (i + 1) % count) for i in range(count)])
    right = lax.ppermute(block[..., :width], "lon", [(i, (i - 1) % count) for i in range(count)])
    return jnp.concatenate([left, block, right], axis=-1)


def coefficients(quadrature, lat_offsets, lon_offsets):
    lat_levels = jnp.arange(2 * LAT_REACH + 1, dtype=jnp.int32)
    lon_levels = jnp.arange(2 * LON_REACH + 1, dtype=jnp.int32)
    lat_onehot = (lat_offsets[..., None] + LAT_REACH == lat_levels).astype(jnp.float32)
    lon_onehot = (lon_offsets[..., None] + LON_REACH == lon_levels).astype(jnp.float32)
    stencil = jnp.einsum(
        "rks,rksa,rksd->krad", quadrature, lat_onehot, lon_onehot, precision=lax.Precision.HIGHEST
    )
    return stencil.astype(jnp.bfloat16)


def lon_picker(col_count):
    span_count = 2 * LON_REACH + 1
    wide_count = col_count + 2 * LON_REACH
    table_shape = (span_count, wide_count, col_count)
    offset_level = lax.broadcasted_iota(jnp.int32, table_shape, 0)
    source = lax.broadcasted_iota(jnp.int32, table_shape, 1)
    target = lax.broadcasted_iota(jnp.int32, table_shape, 2)
    matches = source - target == offset_level
    return matches.astype(jnp.bfloat16)


def band_of(stencil, col_count):
    return jnp.einsum(
        "kiad,dpq->iapkq", stencil, lon_picker(col_count), preferred_element_type=jnp.float32
    ).astype(jnp.bfloat16)


def spread(values, band, basis_count):
    row_count = values.shape[1] - 2 * LAT_REACH
    lat_taps = 2 * LAT_REACH + 1
    stacked = jnp.stack(
        [values[:, offset : offset + row_count] for offset in range(lat_taps)], axis=2
    )
    return jnp.einsum("ciap,iapkq->cikq", stacked, band, preferred_element_type=jnp.float32)


def spread_adjoint(mixed, band):
    row_count, col_count = mixed.shape[1], mixed.shape[3]
    lat_taps = 2 * LAT_REACH + 1
    partial = jnp.einsum("cikq,iapkq->ciap", mixed, band, preferred_element_type=jnp.float32)
    partial = partial[:, :, :, LON_HALO : col_count]
    out_rows = row_count - LAT_HALO
    total = partial[:, LAT_HALO : LAT_HALO + out_rows, 0]
    for offset in range(1, lat_taps):
        start = LAT_HALO - offset
        total = total + partial[:, start : start + out_rows, offset]
    return total


def mix_channels(weight, spreaded):
    return jnp.einsum("koc,cikj->oij", weight, spreaded, preferred_element_type=jnp.float32)


def unmix(weight, grad_rows):
    return jnp.einsum(
        "koc,oij->cikj", weight, grad_rows, preferred_element_type=jnp.float32
    ).astype(jnp.bfloat16)


def filter_term(gradient, spreaded):
    return jnp.einsum("oij,cikj->koc", gradient, spreaded, preferred_element_type=jnp.float32)


def body(state_field, first_weight, second_weight, quadrature, lat_offsets, lon_offsets, cotangent):
    source = state_field[0]
    gradient = cotangent[0]
    channels, row_count, col_count = source.shape
    stencil = coefficients(quadrature, lat_offsets, lon_offsets)
    basis_count = stencil.shape[0]

    packed = jnp.concatenate([source, gradient], axis=0)
    framed = lat_halo(lon_halo(packed, LON_HALO), 1, LAT_HALO)
    source_wide, gradient_wide = framed[:channels], framed[channels:]
    stencil_wide = lat_halo(stencil, 1, LAT_HALO)

    total_rows = row_count * lax.axis_size("lat")
    first_row = lax.axis_index("lat") * row_count
    near_rows = first_row - LAT_REACH + jnp.arange(row_count + 2 * LAT_REACH)
    near_valid = ((near_rows >= 0) & (near_rows < total_rows))[None, :, None]

    near_band = band_of(stencil_wide[:, LAT_REACH : LAT_REACH + row_count + 2 * LAT_REACH], col_count + LON_HALO)
    own_band = band_of(stencil, col_count)
    wide_band = band_of(stencil_wide, col_count + 2 * LON_HALO)

    first_near = spread(source_wide, near_band, basis_count).astype(jnp.bfloat16)
    hidden = mix_channels(first_weight, first_near)
    activation = jnp.where(near_valid, jax.nn.gelu(hidden), 0.0).astype(jnp.bfloat16)
    second_spread = spread(activation, own_band, basis_count).astype(jnp.bfloat16)
    layer_output = mix_channels(second_weight, second_spread).astype(jnp.bfloat16)
    own_gradient = gradient_wide[:, LAT_HALO : LAT_HALO + row_count, LON_HALO : LON_HALO + col_count]
    second_sum = filter_term(own_gradient, second_spread)

    second_mixed = unmix(second_weight, gradient_wide)
    activation_grad = spread_adjoint(second_mixed, wide_band).astype(jnp.bfloat16)
    hidden_grad = jax.vjp(jax.nn.gelu, hidden)[1](activation_grad.astype(jnp.float32))[0]
    hidden_grad = jnp.where(near_valid, hidden_grad, 0.0).astype(jnp.bfloat16)
    own_hidden_grad = hidden_grad[:, LAT_REACH : LAT_REACH + row_count, LON_REACH : LON_REACH + col_count]
    own_first = first_near[:, LAT_REACH : LAT_REACH + row_count, :, LON_REACH : LON_REACH + col_count]
    first_sum = filter_term(own_hidden_grad, own_first)
    first_mixed = unmix(first_weight, hidden_grad)
    state_grad = spread_adjoint(first_mixed, near_band).astype(jnp.bfloat16)

    first_sum, second_sum = jnp.split(
        halving_sum(jnp.concatenate([first_sum, second_sum]), ("ens", "lat", "lon")), 2
    )
    member_total = state_field.shape[0] * lax.axis_size("ens")
    grad_scale = 1.0 / math.sqrt(
        member_total * row_count * lax.axis_size("lat") * col_count * lax.axis_size("lon")
    )
    return (layer_output[None], state_grad[None], first_sum * grad_scale, second_sum * grad_scale)


def solution(mesh):
    in_specs = (
        P("ens", None, "lat", "lon"),
        P(),
        P(),
        P("lat", None, None),
        P("lat", None, None),
        P("lat", None, None),
        P("ens", None, "lat", "lon"),
    )
    out_specs = (P("ens", None, "lat", "lon"), P("ens", None, "lat", "lon"), P(), P())
    return jax.shard_map(body, mesh=mesh, in_specs=in_specs, out_specs=out_specs, check_vma=False)
```

```python
import math

import jax
import jax.numpy as jnp
from jax import lax
from jax.sharding import PartitionSpec as P

LAT_REACH = 1
LON_REACH = 4
LAT_HALO = 2 * LAT_REACH
LON_HALO = 2 * LON_REACH


def halving_sum(value, axes, exchanged=2):
    stages = []
    for axis in axes:
        bit = 1
        while bit < lax.axis_size(axis):
            stages.append((axis, bit))
            bit *= 2
    exchanged = min(exchanged, len(stages))
    halved = stages[: len(stages) - exchanged]
    flat = value.reshape(-1)
    for axis, bit in halved:
        pairs = [(i, i ^ bit) for i in range(lax.axis_size(axis))]
        upper = (lax.axis_index(axis) // bit) % 2
        half = flat.shape[0] // 2
        keep = lax.dynamic_slice_in_dim(flat, upper * half, half)
        send = lax.dynamic_slice_in_dim(flat, (1 - upper) * half, half)
        flat = keep + lax.ppermute(send, axis, pairs)
    for axis, bit in stages[len(halved) :]:
        pairs = [(i, i ^ bit) for i in range(lax.axis_size(axis))]
        flat = flat + lax.ppermute(flat, axis, pairs)
    flat = flat.astype(jnp.bfloat16)
    for axis, bit in reversed(halved):
        pairs = [(i, i ^ bit) for i in range(lax.axis_size(axis))]
        upper = (lax.axis_index(axis) // bit) % 2
        other = lax.ppermute(flat, axis, pairs)
        flat = jnp.where(
            upper == 1, jnp.concatenate([other, flat]), jnp.concatenate([flat, other])
        )
    return flat.astype(jnp.float32).reshape(value.shape)


def lat_halo(block, dim, width):
    count = lax.axis_size("lat")
    rows = block.shape[dim]
    above = lax.ppermute(
        lax.slice_in_dim(block, rows - width, rows, axis=dim),
        "lat",
        [(i, i + 1) for i in range(count - 1)],
    )
    below = lax.ppermute(
        lax.slice_in_dim(block, 0, width, axis=dim), "lat", [(i + 1, i) for i in range(count - 1)]
    )
    return jnp.concatenate([above, block, below], axis=dim)


def lon_halo(block, width):
    count = lax.axis_size("lon")
    cols = block.shape[-1]
    left = lax.ppermute(block[..., cols - width :], "lon", [(i, (i + 1) % count) for i in range(count)])
    right = lax.ppermute(block[..., :width], "lon", [(i, (i - 1) % count) for i in range(count)])
    return jnp.concatenate([left, block, right], axis=-1)


def coefficients(quadrature, lat_offsets, lon_offsets):
    lat_levels = jnp.arange(2 * LAT_REACH + 1, dtype=jnp.int32)
    lon_levels = jnp.arange(2 * LON_REACH + 1, dtype=jnp.int32)
    lat_onehot = (lat_offsets[..., None] + LAT_REACH == lat_levels).astype(jnp.float32)
    lon_onehot = (lon_offsets[..., None] + LON_REACH == lon_levels).astype(jnp.float32)
    stencil = jnp.einsum(
        "rks,rksa,rksd->krad", quadrature, lat_onehot, lon_onehot, precision=lax.Precision.HIGHEST
    )
    return stencil.astype(jnp.bfloat16)


def lon_picker(col_count):
    span_count = 2 * LON_REACH + 1
    wide_count = col_count + 2 * LON_REACH
    table_shape = (span_count, wide_count, col_count)
    offset_level = lax.broadcasted_iota(jnp.int32, table_shape, 0)
    source = lax.broadcasted_iota(jnp.int32, table_shape, 1)
    target = lax.broadcasted_iota(jnp.int32, table_shape, 2)
    matches = source - target == offset_level
    return matches.astype(jnp.bfloat16)


def band_of(stencil, col_count):
    return jnp.einsum(
        "kiad,dpq->iapkq", stencil, lon_picker(col_count), preferred_element_type=jnp.float32
    ).astype(jnp.bfloat16)


def spread(values, band, basis_count):
    row_count = values.shape[1] - 2 * LAT_REACH
    lat_taps = 2 * LAT_REACH + 1
    stacked = jnp.stack(
        [values[:, offset : offset + row_count] for offset in range(lat_taps)], axis=2
    )
    return jnp.einsum("ciap,iapkq->cikq", stacked, band, preferred_element_type=jnp.float32)


def spread_adjoint(mixed, band):
    row_count, col_count = mixed.shape[1], mixed.shape[3]
    lat_taps = 2 * LAT_REACH + 1
    partial = jnp.einsum("cikq,iapkq->ciap", mixed, band, preferred_element_type=jnp.float32)
    partial = partial[:, :, :, LON_HALO : col_count]
    out_rows = row_count - LAT_HALO
    total = partial[:, LAT_HALO : LAT_HALO + out_rows, 0]
    for offset in range(1, lat_taps):
        start = LAT_HALO - offset
        total = total + partial[:, start : start + out_rows, offset]
    return total


def mix_channels(weight, spreaded):
    return jnp.einsum("koc,cikj->oij", weight, spreaded, preferred_element_type=jnp.float32)


def unmix(weight, grad_rows):
    return jnp.einsum(
        "koc,oij->cikj", weight, grad_rows, preferred_element_type=jnp.float32
    ).astype(jnp.bfloat16)


def filter_term(gradient, spreaded):
    return jnp.einsum("oij,cikj->koc", gradient, spreaded, preferred_element_type=jnp.float32)


def body(state_field, first_weight, second_weight, quadrature, lat_offsets, lon_offsets, cotangent):
    source = state_field[0]
    gradient = cotangent[0]
    channels, row_count, col_count = source.shape
    stencil = coefficients(quadrature, lat_offsets, lon_offsets)
    basis_count = stencil.shape[0]

    packed = lon_halo(jnp.concatenate([source, gradient], axis=0), LON_HALO)
    taps_per_row = stencil.size // row_count
    stencil_rows = jnp.transpose(stencil, (1, 0, 2, 3)).reshape(row_count, taps_per_row)
    stencil_rows = jnp.pad(stencil_rows, ((0, 0), (0, packed.shape[2] - taps_per_row)))
    framed = lat_halo(jnp.concatenate([packed, stencil_rows[None]], axis=0), 1, LAT_HALO)
    source_wide, gradient_wide = framed[:channels], framed[channels : 2 * channels]
    stencil_wide = framed[2 * channels, :, :taps_per_row].reshape(
        row_count + 2 * LAT_HALO, stencil.shape[0], stencil.shape[2], stencil.shape[3]
    )
    stencil_wide = jnp.transpose(stencil_wide, (1, 0, 2, 3))

    total_rows = row_count * lax.axis_size("lat")
    first_row = lax.axis_index("lat") * row_count
    near_rows = first_row - LAT_REACH + jnp.arange(row_count + 2 * LAT_REACH)
    near_valid = ((near_rows >= 0) & (near_rows < total_rows))[None, :, None]

    near_band = band_of(stencil_wide[:, LAT_REACH : LAT_REACH + row_count + 2 * LAT_REACH], col_count + LON_HALO)
    own_band = band_of(stencil, col_count)
    wide_band = band_of(stencil_wide, col_count + 2 * LON_HALO)

    first_near = spread(source_wide, near_band, basis_count).astype(jnp.bfloat16)
    hidden = mix_channels(first_weight, first_near)
    activation = jnp.where(near_valid, jax.nn.gelu(hidden), 0.0).astype(jnp.bfloat16)
    second_spread = spread(activation, own_band, basis_count).astype(jnp.bfloat16)
    layer_output = mix_channels(second_weight, second_spread).astype(jnp.bfloat16)
    own_gradient = gradient_wide[:, LAT_HALO : LAT_HALO + row_count, LON_HALO : LON_HALO + col_count]
    second_sum = filter_term(own_gradient, second_spread)

    second_mixed = unmix(second_weight, gradient_wide)
    activation_grad = spread_adjoint(second_mixed, wide_band).astype(jnp.bfloat16)
    hidden_grad = jax.vjp(jax.nn.gelu, hidden)[1](activation_grad.astype(jnp.float32))[0]
    hidden_grad = jnp.where(near_valid, hidden_grad, 0.0).astype(jnp.bfloat16)
    own_hidden_grad = hidden_grad[:, LAT_REACH : LAT_REACH + row_count, LON_REACH : LON_REACH + col_count]
    own_first = first_near[:, LAT_REACH : LAT_REACH + row_count, :, LON_REACH : LON_REACH + col_count]
    first_sum = filter_term(own_hidden_grad, own_first)
    first_mixed = unmix(first_weight, hidden_grad)
    state_grad = spread_adjoint(first_mixed, near_band).astype(jnp.bfloat16)

    first_sum, second_sum = jnp.split(
        halving_sum(jnp.concatenate([first_sum, second_sum]), ("ens", "lat", "lon")), 2
    )
    member_total = state_field.shape[0] * lax.axis_size("ens")
    grad_scale = 1.0 / math.sqrt(
        member_total * row_count * lax.axis_size("lat") * col_count * lax.axis_size("lon")
    )
    return (layer_output[None], state_grad[None], first_sum * grad_scale, second_sum * grad_scale)


def solution(mesh):
    in_specs = (
        P("ens", None, "lat", "lon"),
        P(),
        P(),
        P("lat", None, None),
        P("lat", None, None),
        P("lat", None, None),
        P("ens", None, "lat", "lon"),
    )
    out_specs = (P("ens", None, "lat", "lon"), P("ens", None, "lat", "lon"), P(), P())
    return jax.shard_map(body, mesh=mesh, in_specs=in_specs, out_specs=out_specs, check_vma=False)
```

```python
import math

import jax
import jax.numpy as jnp
from jax import lax
from jax.sharding import PartitionSpec as P

LAT_REACH = 1
LON_REACH = 4
LAT_HALO = 2 * LAT_REACH
LON_HALO = 2 * LON_REACH


def halving_sum(value, axes, exchanged=2):
    stages = []
    for axis in axes:
        bit = 1
        while bit < lax.axis_size(axis):
            stages.append((axis, bit))
            bit *= 2
    exchanged = min(exchanged, len(stages))
    halved = stages[: len(stages) - exchanged]
    flat = value.reshape(-1)
    for axis, bit in halved:
        pairs = [(i, i ^ bit) for i in range(lax.axis_size(axis))]
        upper = (lax.axis_index(axis) // bit) % 2
        half = flat.shape[0] // 2
        keep = lax.dynamic_slice_in_dim(flat, upper * half, half)
        send = lax.dynamic_slice_in_dim(flat, (1 - upper) * half, half)
        flat = keep + lax.ppermute(send, axis, pairs)
    for axis, bit in stages[len(halved) :]:
        pairs = [(i, i ^ bit) for i in range(lax.axis_size(axis))]
        flat = flat + lax.ppermute(flat, axis, pairs)
    flat = flat.astype(jnp.bfloat16)
    for axis, bit in reversed(halved):
        pairs = [(i, i ^ bit) for i in range(lax.axis_size(axis))]
        upper = (lax.axis_index(axis) // bit) % 2
        other = lax.ppermute(flat, axis, pairs)
        flat = jnp.where(
            upper == 1, jnp.concatenate([other, flat]), jnp.concatenate([flat, other])
        )
    return flat.astype(jnp.float32).reshape(value.shape)


def lat_halo(block, dim, width):
    count = lax.axis_size("lat")
    rows = block.shape[dim]
    above = lax.ppermute(
        lax.slice_in_dim(block, rows - width, rows, axis=dim),
        "lat",
        [(i, i + 1) for i in range(count - 1)],
    )
    below = lax.ppermute(
        lax.slice_in_dim(block, 0, width, axis=dim), "lat", [(i + 1, i) for i in range(count - 1)]
    )
    return jnp.concatenate([above, block, below], axis=dim)


def lon_halo(block, width):
    count = lax.axis_size("lon")
    cols = block.shape[-1]
    left = lax.ppermute(block[..., cols - width :], "lon", [(i, (i + 1) % count) for i in range(count)])
    right = lax.ppermute(block[..., :width], "lon", [(i, (i - 1) % count) for i in range(count)])
    return jnp.concatenate([left, block, right], axis=-1)


def coefficients(quadrature, lat_offsets, lon_offsets):
    lat_levels = jnp.arange(2 * LAT_REACH + 1, dtype=jnp.int32)
    lon_levels = jnp.arange(2 * LON_REACH + 1, dtype=jnp.int32)
    lat_onehot = (lat_offsets[..., None] + LAT_REACH == lat_levels).astype(jnp.float32)
    lon_onehot = (lon_offsets[..., None] + LON_REACH == lon_levels).astype(jnp.float32)
    stencil = jnp.einsum(
        "rks,rksa,rksd->krad", quadrature, lat_onehot, lon_onehot, precision=lax.Precision.HIGHEST
    )
    return stencil.astype(jnp.bfloat16)


def lon_picker(col_count):
    span_count = 2 * LON_REACH + 1
    wide_count = col_count + 2 * LON_REACH
    table_shape = (span_count, wide_count, col_count)
    offset_level = lax.broadcasted_iota(jnp.int32, table_shape, 0)
    source = lax.broadcasted_iota(jnp.int32, table_shape, 1)
    target = lax.broadcasted_iota(jnp.int32, table_shape, 2)
    matches = source - target == offset_level
    return matches.astype(jnp.bfloat16)


def band_of(stencil, col_count):
    return jnp.einsum(
        "kiad,dpq->iapkq", stencil, lon_picker(col_count), preferred_element_type=jnp.float32
    ).astype(jnp.bfloat16)


def spread(values, band, basis_count):
    row_count = values.shape[1] - 2 * LAT_REACH
    lat_taps = 2 * LAT_REACH + 1
    stacked = jnp.stack(
        [values[:, offset : offset + row_count] for offset in range(lat_taps)], axis=2
    )
    return jnp.einsum("ciap,iapkq->cikq", stacked, band, preferred_element_type=jnp.float32)


def spread_adjoint(mixed, band):
    row_count, col_count = mixed.shape[1], mixed.shape[3]
    lat_taps = 2 * LAT_REACH + 1
    partial = jnp.einsum("cikq,iapkq->ciap", mixed, band, preferred_element_type=jnp.float32)
    partial = partial[:, :, :, LON_HALO : col_count]
    out_rows = row_count - LAT_HALO
    total = partial[:, LAT_HALO : LAT_HALO + out_rows, 0]
    for offset in range(1, lat_taps):
        start = LAT_HALO - offset
        total = total + partial[:, start : start + out_rows, offset]
    return total


def mix_channels(weight, spreaded):
    return jnp.einsum("koc,cikj->oij", weight, spreaded, preferred_element_type=jnp.float32)


def unmix(weight, grad_rows):
    return jnp.einsum(
        "koc,oij->cikj", weight, grad_rows, preferred_element_type=jnp.float32
    ).astype(jnp.bfloat16)


def filter_term(gradient, spreaded):
    return jnp.einsum("oij,cikj->koc", gradient, spreaded, preferred_element_type=jnp.float32)


def body(state_field, first_weight, second_weight, quadrature, lat_offsets, lon_offsets, cotangent):
    source = state_field[0]
    gradient = cotangent[0]
    channels, row_count, col_count = source.shape
    stencil = coefficients(quadrature, lat_offsets, lon_offsets)
    basis_count = stencil.shape[0]

    packed = lon_halo(jnp.concatenate([source, gradient], axis=0), LON_HALO)
    taps_per_row = stencil.size // row_count
    stencil_rows = jnp.transpose(stencil, (1, 0, 2, 3)).reshape(row_count, taps_per_row)
    stencil_rows = jnp.pad(stencil_rows, ((0, 0), (0, packed.shape[2] - taps_per_row)))
    framed = lat_halo(jnp.concatenate([packed, stencil_rows[None]], axis=0), 1, LAT_HALO)
    source_wide, gradient_wide = framed[:channels], framed[channels : 2 * channels]
    stencil_wide = framed[2 * channels, :, :taps_per_row].reshape(
        row_count + 2 * LAT_HALO, stencil.shape[0], stencil.shape[2], stencil.shape[3]
    )
    stencil_wide = jnp.transpose(stencil_wide, (1, 0, 2, 3))

    total_rows = row_count * lax.axis_size("lat")
    first_row = lax.axis_index("lat") * row_count
    near_rows = first_row - LAT_REACH + jnp.arange(row_count + 2 * LAT_REACH)
    near_valid = ((near_rows >= 0) & (near_rows < total_rows))[None, :, None]

    near_band = band_of(stencil_wide[:, LAT_REACH : LAT_REACH + row_count + 2 * LAT_REACH], col_count + LON_HALO)
    own_band = band_of(stencil, col_count)
    wide_band = band_of(stencil_wide, col_count + 2 * LON_HALO)

    first_near = spread(source_wide, near_band, basis_count).astype(jnp.bfloat16)
    hidden = mix_channels(first_weight, first_near)
    activation = jnp.where(near_valid, jax.nn.gelu(hidden), 0.0).astype(jnp.bfloat16)
    second_spread = spread(activation, own_band, basis_count).astype(jnp.bfloat16)
    layer_output = mix_channels(second_weight, second_spread).astype(jnp.bfloat16)
    own_gradient = gradient_wide[:, LAT_HALO : LAT_HALO + row_count, LON_HALO : LON_HALO + col_count]
    second_sum = filter_term(own_gradient, second_spread)

    second_mixed = unmix(second_weight, gradient_wide)
    activation_grad = spread_adjoint(second_mixed, wide_band).astype(jnp.bfloat16)
    hidden_grad = jax.vjp(jax.nn.gelu, hidden)[1](activation_grad.astype(jnp.float32))[0]
    hidden_grad = jnp.where(near_valid, hidden_grad, 0.0).astype(jnp.bfloat16)
    own_hidden_grad = hidden_grad[:, LAT_REACH : LAT_REACH + row_count, LON_REACH : LON_REACH + col_count]
    own_first = first_near[:, LAT_REACH : LAT_REACH + row_count, :, LON_REACH : LON_REACH + col_count]
    first_sum = filter_term(own_hidden_grad, own_first)
    first_mixed = unmix(first_weight, hidden_grad)
    state_grad = spread_adjoint(first_mixed, near_band).astype(jnp.bfloat16)

    member_total = state_field.shape[0] * lax.axis_size("ens")
    grad_scale = 1.0 / math.sqrt(
        member_total * row_count * lax.axis_size("lat") * col_count * lax.axis_size("lon")
    )
    first_grad = halving_sum(first_sum * grad_scale, ("ens", "lat", "lon"))
    second_grad = halving_sum(second_sum * grad_scale, ("ens", "lat", "lon"))
    return (layer_output[None], state_grad[None], first_grad, second_grad)


def solution(mesh):
    in_specs = (
        P("ens", None, "lat", "lon"),
        P(),
        P(),
        P("lat", None, None),
        P("lat", None, None),
        P("lat", None, None),
        P("ens", None, "lat", "lon"),
    )
    out_specs = (P("ens", None, "lat", "lon"), P("ens", None, "lat", "lon"), P(), P())
    return jax.shard_map(body, mesh=mesh, in_specs=in_specs, out_specs=out_specs, check_vma=False)
```

```python
import math

import jax
import jax.numpy as jnp
from jax import lax
from jax.sharding import PartitionSpec as P

LAT_REACH = 1
LON_REACH = 4
LAT_HALO = 2 * LAT_REACH
LON_HALO = 2 * LON_REACH


def halving_sum(value, axes, exchanged=2, hold=None):
    stages = []
    for axis in axes:
        bit = 1
        while bit < lax.axis_size(axis):
            stages.append((axis, bit))
            bit *= 2
    exchanged = min(exchanged, len(stages))
    halved = stages[: len(stages) - exchanged]
    flat = value.reshape(-1)
    held = hold
    for axis, bit in halved:
        pairs = [(i, i ^ bit) for i in range(lax.axis_size(axis))]
        upper = (lax.axis_index(axis) // bit) % 2
        half = flat.shape[0] // 2
        keep = lax.dynamic_slice_in_dim(flat, upper * half, half)
        send = lax.dynamic_slice_in_dim(flat, (1 - upper) * half, half)
        flat = keep + lax.ppermute(send, axis, pairs)
        if hold is not None:
            flat, hold = lax.optimization_barrier((flat, hold))
            held, hold = hold, None
    for axis, bit in stages[len(halved) :]:
        pairs = [(i, i ^ bit) for i in range(lax.axis_size(axis))]
        flat = flat + lax.ppermute(flat, axis, pairs)
    flat = flat.astype(jnp.bfloat16)
    for axis, bit in reversed(halved):
        pairs = [(i, i ^ bit) for i in range(lax.axis_size(axis))]
        upper = (lax.axis_index(axis) // bit) % 2
        other = lax.ppermute(flat, axis, pairs)
        flat = jnp.where(
            upper == 1, jnp.concatenate([other, flat]), jnp.concatenate([flat, other])
        )
    return flat.astype(jnp.float32).reshape(value.shape), held


def lat_halo(block, dim, width):
    count = lax.axis_size("lat")
    rows = block.shape[dim]
    above = lax.ppermute(
        lax.slice_in_dim(block, rows - width, rows, axis=dim),
        "lat",
        [(i, i + 1) for i in range(count - 1)],
    )
    below = lax.ppermute(
        lax.slice_in_dim(block, 0, width, axis=dim), "lat", [(i + 1, i) for i in range(count - 1)]
    )
    return jnp.concatenate([above, block, below], axis=dim)


def lon_halo(block, width):
    count = lax.axis_size("lon")
    cols = block.shape[-1]
    left = lax.ppermute(block[..., cols - width :], "lon", [(i, (i + 1) % count) for i in range(count)])
    right = lax.ppermute(block[..., :width], "lon", [(i, (i - 1) % count) for i in range(count)])
    return jnp.concatenate([left, block, right], axis=-1)


def coefficients(quadrature, lat_offsets, lon_offsets):
    lat_levels = jnp.arange(2 * LAT_REACH + 1, dtype=jnp.int32)
    lon_levels = jnp.arange(2 * LON_REACH + 1, dtype=jnp.int32)
    lat_onehot = (lat_offsets[..., None] + LAT_REACH == lat_levels).astype(jnp.float32)
    lon_onehot = (lon_offsets[..., None] + LON_REACH == lon_levels).astype(jnp.float32)
    stencil = jnp.einsum(
        "rks,rksa,rksd->krad", quadrature, lat_onehot, lon_onehot, precision=lax.Precision.HIGHEST
    )
    return stencil.astype(jnp.bfloat16)


def lon_picker(col_count, first_source=0, source_count=None):
    span_count = 2 * LON_REACH + 1
    if source_count is None:
        source_count = col_count + 2 * LON_REACH
    table_shape = (span_count, source_count, col_count)
    offset_level = lax.broadcasted_iota(jnp.int32, table_shape, 0)
    source = lax.broadcasted_iota(jnp.int32, table_shape, 1) + first_source
    target = lax.broadcasted_iota(jnp.int32, table_shape, 2)
    matches = source - target == offset_level
    return matches.astype(jnp.bfloat16)


def band_of(stencil, col_count, first_source=0, source_count=None):
    return jnp.einsum(
        "kiad,dpq->iapkq",
        stencil,
        lon_picker(col_count, first_source, source_count),
        preferred_element_type=jnp.float32,
    ).astype(jnp.bfloat16)


def spread(values, band, basis_count):
    row_count = values.shape[1] - 2 * LAT_REACH
    lat_taps = 2 * LAT_REACH + 1
    stacked = jnp.stack(
        [values[:, offset : offset + row_count] for offset in range(lat_taps)], axis=2
    )
    return jnp.einsum("ciap,iapkq->cikq", stacked, band, preferred_element_type=jnp.float32)


def spread_adjoint(mixed, band):
    row_count, col_count = mixed.shape[1], mixed.shape[3]
    lat_taps = 2 * LAT_REACH + 1
    partial = jnp.einsum("cikq,iapkq->ciap", mixed, band, preferred_element_type=jnp.float32)
    if partial.shape[3] != col_count - LON_HALO:
        partial = partial[:, :, :, LON_HALO : col_count]
    out_rows = row_count - LAT_HALO
    total = partial[:, LAT_HALO : LAT_HALO + out_rows, 0]
    for offset in range(1, lat_taps):
        start = LAT_HALO - offset
        total = total + partial[:, start : start + out_rows, offset]
    return total


def mix_channels(weight, spreaded):
    return jnp.einsum("koc,cikj->oij", weight, spreaded, preferred_element_type=jnp.float32)


def unmix(weight, grad_rows):
    return jnp.einsum(
        "koc,oij->cikj", weight, grad_rows, preferred_element_type=jnp.float32
    ).astype(jnp.bfloat16)


def filter_term(gradient, spreaded):
    return jnp.einsum("oij,cikj->koc", gradient, spreaded, preferred_element_type=jnp.float32)


def body(state_field, first_weight, second_weight, quadrature, lat_offsets, lon_offsets, cotangent):
    source = state_field[0]
    gradient = cotangent[0]
    channels, row_count, col_count = source.shape
    stencil = coefficients(quadrature, lat_offsets, lon_offsets)
    basis_count = stencil.shape[0]

    packed = lon_halo(jnp.concatenate([source, gradient], axis=0), LON_HALO)
    taps_per_row = stencil.size // row_count
    stencil_rows = jnp.transpose(stencil, (1, 0, 2, 3)).reshape(row_count, taps_per_row)
    stencil_rows = jnp.pad(stencil_rows, ((0, 0), (0, packed.shape[2] - taps_per_row)))
    framed = lat_halo(jnp.concatenate([packed, stencil_rows[None]], axis=0), 1, LAT_HALO)
    source_wide, gradient_wide = framed[:channels], framed[channels : 2 * channels]
    stencil_wide = framed[2 * channels, :, :taps_per_row].reshape(
        row_count + 2 * LAT_HALO, stencil.shape[0], stencil.shape[2], stencil.shape[3]
    )
    stencil_wide = jnp.transpose(stencil_wide, (1, 0, 2, 3))

    total_rows = row_count * lax.axis_size("lat")
    first_row = lax.axis_index("lat") * row_count
    near_rows = first_row - LAT_REACH + jnp.arange(row_count + 2 * LAT_REACH)
    near_valid = ((near_rows >= 0) & (near_rows < total_rows))[None, :, None]

    near_band = band_of(stencil_wide[:, LAT_REACH : LAT_REACH + row_count + 2 * LAT_REACH], col_count + LON_HALO)
    own_band = band_of(stencil, col_count)
    wide_band = band_of(stencil_wide, col_count + 2 * LON_HALO, LON_HALO, col_count + LON_HALO)

    first_near = spread(source_wide, near_band, basis_count).astype(jnp.bfloat16)
    hidden = mix_channels(first_weight, first_near)
    activation = jnp.where(near_valid, jax.nn.gelu(hidden), 0.0).astype(jnp.bfloat16)
    second_spread = spread(activation, own_band, basis_count).astype(jnp.bfloat16)
    own_gradient = gradient_wide[:, LAT_HALO : LAT_HALO + row_count, LON_HALO : LON_HALO + col_count]
    second_sum = filter_term(own_gradient, second_spread)

    second_mixed = unmix(second_weight, gradient_wide)
    activation_grad = spread_adjoint(second_mixed, wide_band).astype(jnp.bfloat16)
    hidden_grad = jax.vjp(jax.nn.gelu, hidden)[1](activation_grad.astype(jnp.float32))[0]
    hidden_grad = jnp.where(near_valid, hidden_grad, 0.0).astype(jnp.bfloat16)
    own_hidden_grad = hidden_grad[:, LAT_REACH : LAT_REACH + row_count, LON_REACH : LON_REACH + col_count]
    own_first = first_near[:, LAT_REACH : LAT_REACH + row_count, :, LON_REACH : LON_REACH + col_count]
    first_sum = filter_term(own_hidden_grad, own_first)
    member_total = state_field.shape[0] * lax.axis_size("ens")
    grad_scale = 1.0 / math.sqrt(
        member_total * row_count * lax.axis_size("lat") * col_count * lax.axis_size("lon")
    )
    axes = ("ens", "lat", "lon")
    second_grad, second_spread = halving_sum(second_sum * grad_scale, axes, hold=second_spread)
    first_grad, hidden_grad = halving_sum(first_sum * grad_scale, axes, hold=hidden_grad)
    layer_output = mix_channels(second_weight, second_spread).astype(jnp.bfloat16)
    first_mixed = unmix(first_weight, hidden_grad)
    state_grad = spread_adjoint(first_mixed, near_band).astype(jnp.bfloat16)
    return (layer_output[None], state_grad[None], first_grad, second_grad)


def solution(mesh):
    in_specs = (
        P("ens", None, "lat", "lon"),
        P(),
        P(),
        P("lat", None, None),
        P("lat", None, None),
        P("lat", None, None),
        P("ens", None, "lat", "lon"),
    )
    out_specs = (P("ens", None, "lat", "lon"), P("ens", None, "lat", "lon"), P(), P())
    return jax.shard_map(body, mesh=mesh, in_specs=in_specs, out_specs=out_specs, check_vma=False)
```

```python
import math

import jax
import jax.numpy as jnp
from jax import lax
from jax.sharding import PartitionSpec as P

LAT_REACH = 1
LON_REACH = 4
LAT_HALO = 2 * LAT_REACH
LON_HALO = 2 * LON_REACH


def halving_sum(value, axes, exchanged=2, hold=None):
    stages = []
    for axis in axes:
        bit = 1
        while bit < lax.axis_size(axis):
            stages.append((axis, bit))
            bit *= 2
    exchanged = min(exchanged, len(stages))
    halved = stages[: len(stages) - exchanged]
    flat = value.reshape(-1, value.shape[-1])
    held = hold
    for axis, bit in halved:
        pairs = [(i, i ^ bit) for i in range(lax.axis_size(axis))]
        upper = (lax.axis_index(axis) // bit) % 2
        half = flat.shape[0] // 2
        keep = lax.dynamic_slice_in_dim(flat, upper * half, half)
        send = lax.dynamic_slice_in_dim(flat, (1 - upper) * half, half)
        flat = keep + lax.ppermute(send, axis, pairs)
        if hold is not None:
            flat, hold = lax.optimization_barrier((flat, hold))
            held, hold = hold, None
    for axis, bit in stages[len(halved) :]:
        pairs = [(i, i ^ bit) for i in range(lax.axis_size(axis))]
        flat = flat + lax.ppermute(flat, axis, pairs)
    flat = flat.astype(jnp.bfloat16)
    for axis, bit in reversed(halved):
        pairs = [(i, i ^ bit) for i in range(lax.axis_size(axis))]
        upper = (lax.axis_index(axis) // bit) % 2
        other = lax.ppermute(flat, axis, pairs)
        flat = jnp.where(
            upper == 1, jnp.concatenate([other, flat]), jnp.concatenate([flat, other])
        )
    return flat.astype(jnp.float32).reshape(value.shape), held


def lat_halo(block, dim, width):
    count = lax.axis_size("lat")
    rows = block.shape[dim]
    above = lax.ppermute(
        lax.slice_in_dim(block, rows - width, rows, axis=dim),
        "lat",
        [(i, i + 1) for i in range(count - 1)],
    )
    below = lax.ppermute(
        lax.slice_in_dim(block, 0, width, axis=dim), "lat", [(i + 1, i) for i in range(count - 1)]
    )
    return jnp.concatenate([above, block, below], axis=dim)


def lon_halo(block, width):
    count = lax.axis_size("lon")
    cols = block.shape[-1]
    left = lax.ppermute(block[..., cols - width :], "lon", [(i, (i + 1) % count) for i in range(count)])
    right = lax.ppermute(block[..., :width], "lon", [(i, (i - 1) % count) for i in range(count)])
    return jnp.concatenate([left, block, right], axis=-1)


def coefficients(quadrature, lat_offsets, lon_offsets):
    lat_levels = jnp.arange(2 * LAT_REACH + 1, dtype=jnp.int32)
    lon_levels = jnp.arange(2 * LON_REACH + 1, dtype=jnp.int32)
    lat_onehot = (lat_offsets[..., None] + LAT_REACH == lat_levels).astype(jnp.float32)
    lon_onehot = (lon_offsets[..., None] + LON_REACH == lon_levels).astype(jnp.float32)
    stencil = jnp.einsum(
        "rks,rksa,rksd->krad", quadrature, lat_onehot, lon_onehot, precision=lax.Precision.HIGHEST
    )
    return stencil.astype(jnp.bfloat16)


def lon_picker(col_count, first_source=0, source_count=None):
    span_count = 2 * LON_REACH + 1
    if source_count is None:
        source_count = col_count + 2 * LON_REACH
    table_shape = (span_count, source_count, col_count)
    offset_level = lax.broadcasted_iota(jnp.int32, table_shape, 0)
    source = lax.broadcasted_iota(jnp.int32, table_shape, 1) + first_source
    target = lax.broadcasted_iota(jnp.int32, table_shape, 2)
    matches = source - target == offset_level
    return matches.astype(jnp.bfloat16)


def band_of(stencil, col_count, first_source=0, source_count=None):
    return jnp.einsum(
        "kiad,dpq->iapkq",
        stencil,
        lon_picker(col_count, first_source, source_count),
        preferred_element_type=jnp.float32,
    ).astype(jnp.bfloat16)


def spread(values, band, basis_count):
    row_count = values.shape[1] - 2 * LAT_REACH
    lat_taps = 2 * LAT_REACH + 1
    stacked = jnp.stack(
        [values[:, offset : offset + row_count] for offset in range(lat_taps)], axis=2
    )
    return jnp.einsum("ciap,iapkq->cikq", stacked, band, preferred_element_type=jnp.float32)


def spread_adjoint(mixed, band):
    row_count, col_count = mixed.shape[1], mixed.shape[3]
    lat_taps = 2 * LAT_REACH + 1
    partial = jnp.einsum("cikq,iapkq->ciap", mixed, band, preferred_element_type=jnp.float32)
    if partial.shape[3] != col_count - LON_HALO:
        partial = partial[:, :, :, LON_HALO : col_count]
    out_rows = row_count - LAT_HALO
    total = partial[:, LAT_HALO : LAT_HALO + out_rows, 0]
    for offset in range(1, lat_taps):
        start = LAT_HALO - offset
        total = total + partial[:, start : start + out_rows, offset]
    return total


def mix_channels(weight, spreaded):
    return jnp.einsum("koc,cikj->oij", weight, spreaded, preferred_element_type=jnp.float32)


def unmix(weight, grad_rows):
    return jnp.einsum(
        "koc,oij->cikj", weight, grad_rows, preferred_element_type=jnp.float32
    ).astype(jnp.bfloat16)


def filter_term(gradient, spreaded):
    return jnp.einsum("oij,cikj->koc", gradient, spreaded, preferred_element_type=jnp.float32)


def body(state_field, first_weight, second_weight, quadrature, lat_offsets, lon_offsets, cotangent):
    source = state_field[0]
    gradient = cotangent[0]
    channels, row_count, col_count = source.shape
    stencil = coefficients(quadrature, lat_offsets, lon_offsets)
    basis_count = stencil.shape[0]

    packed = lon_halo(jnp.concatenate([source, gradient], axis=0), LON_HALO)
    taps_per_row = stencil.size // row_count
    stencil_rows = jnp.transpose(stencil, (1, 0, 2, 3)).reshape(row_count, taps_per_row)
    stencil_rows = jnp.pad(stencil_rows, ((0, 0), (0, packed.shape[2] - taps_per_row)))
    framed = lat_halo(jnp.concatenate([packed, stencil_rows[None]], axis=0), 1, LAT_HALO)
    source_wide, gradient_wide = framed[:channels], framed[channels : 2 * channels]
    stencil_wide = framed[2 * channels, :, :taps_per_row].reshape(
        row_count + 2 * LAT_HALO, stencil.shape[0], stencil.shape[2], stencil.shape[3]
    )
    stencil_wide = jnp.transpose(stencil_wide, (1, 0, 2, 3))

    total_rows = row_count * lax.axis_size("lat")
    first_row = lax.axis_index("lat") * row_count
    near_rows = first_row - LAT_REACH + jnp.arange(row_count + 2 * LAT_REACH)
    near_valid = ((near_rows >= 0) & (near_rows < total_rows))[None, :, None]

    near_band = band_of(stencil_wide[:, LAT_REACH : LAT_REACH + row_count + 2 * LAT_REACH], col_count + LON_HALO)
    own_band = band_of(stencil, col_count)
    wide_band = band_of(stencil_wide, col_count + 2 * LON_HALO, LON_HALO, col_count + LON_HALO)

    first_near = spread(source_wide, near_band, basis_count).astype(jnp.bfloat16)
    hidden = mix_channels(first_weight, first_near)
    activation = jnp.where(near_valid, jax.nn.gelu(hidden), 0.0).astype(jnp.bfloat16)
    second_spread = spread(activation, own_band, basis_count).astype(jnp.bfloat16)
    own_gradient = gradient_wide[:, LAT_HALO : LAT_HALO + row_count, LON_HALO : LON_HALO + col_count]
    second_sum = filter_term(own_gradient, second_spread)

    second_mixed = unmix(second_weight, gradient_wide)
    activation_grad = spread_adjoint(second_mixed, wide_band).astype(jnp.bfloat16)
    hidden_grad = jax.vjp(jax.nn.gelu, hidden)[1](activation_grad.astype(jnp.float32))[0]
    hidden_grad = jnp.where(near_valid, hidden_grad, 0.0).astype(jnp.bfloat16)
    own_hidden_grad = hidden_grad[:, LAT_REACH : LAT_REACH + row_count, LON_REACH : LON_REACH + col_count]
    own_first = first_near[:, LAT_REACH : LAT_REACH + row_count, :, LON_REACH : LON_REACH + col_count]
    first_sum = filter_term(own_hidden_grad, own_first)
    member_total = state_field.shape[0] * lax.axis_size("ens")
    grad_scale = 1.0 / math.sqrt(
        member_total * row_count * lax.axis_size("lat") * col_count * lax.axis_size("lon")
    )
    axes = ("ens", "lat", "lon")
    second_grad, second_spread = halving_sum(second_sum * grad_scale, axes, hold=second_spread)
    first_grad, hidden_grad = halving_sum(first_sum * grad_scale, axes, hold=hidden_grad)
    layer_output = mix_channels(second_weight, second_spread).astype(jnp.bfloat16)
    first_mixed = unmix(first_weight, hidden_grad)
    state_grad = spread_adjoint(first_mixed, near_band).astype(jnp.bfloat16)
    return (layer_output[None], state_grad[None], first_grad, second_grad)


def solution(mesh):
    in_specs = (
        P("ens", None, "lat", "lon"),
        P(),
        P(),
        P("lat", None, None),
        P("lat", None, None),
        P("lat", None, None),
        P("ens", None, "lat", "lon"),
    )
    out_specs = (P("ens", None, "lat", "lon"), P("ens", None, "lat", "lon"), P(), P())
    return jax.shard_map(body, mesh=mesh, in_specs=in_specs, out_specs=out_specs, check_vma=False)
```

```python
import math

import jax
import jax.numpy as jnp
from jax import lax
from jax.sharding import PartitionSpec as P

LAT_REACH = 1
LON_REACH = 4
LAT_HALO = 2 * LAT_REACH
LON_HALO = 2 * LON_REACH


def halving_sum(value, axes, exchanged=2, hold=None):
    stages = []
    for axis in axes:
        bit = 1
        while bit < lax.axis_size(axis):
            stages.append((axis, bit))
            bit *= 2
    exchanged = min(exchanged, len(stages))
    halved = stages[: len(stages) - exchanged]
    flat = value.reshape(-1, value.shape[-1])
    held = hold
    for axis, bit in halved:
        pairs = [(i, i ^ bit) for i in range(lax.axis_size(axis))]
        upper = (lax.axis_index(axis) // bit) % 2
        half = flat.shape[0] // 2
        keep = lax.dynamic_slice_in_dim(flat, upper * half, half)
        send = lax.dynamic_slice_in_dim(flat, (1 - upper) * half, half)
        flat = keep + lax.ppermute(send, axis, pairs)
        if hold is not None:
            flat, hold = lax.optimization_barrier((flat, hold))
            held, hold = hold, None
    for axis, bit in stages[len(halved) :]:
        pairs = [(i, i ^ bit) for i in range(lax.axis_size(axis))]
        flat = flat + lax.ppermute(flat, axis, pairs)
    flat = flat.astype(jnp.bfloat16)
    for axis, bit in reversed(halved):
        pairs = [(i, i ^ bit) for i in range(lax.axis_size(axis))]
        upper = (lax.axis_index(axis) // bit) % 2
        other = lax.ppermute(flat, axis, pairs)
        flat = jnp.where(
            upper == 1, jnp.concatenate([other, flat]), jnp.concatenate([flat, other])
        )
    return flat.astype(jnp.float32).reshape(value.shape), held


def neighbour_piece(block, lat_step, lon_step, lat_width, lon_width):
    lat_count, lon_count = lax.axis_size("lat"), lax.axis_size("lon")
    rows, cols = block.shape[1], block.shape[2]
    if lat_step:
        block = block[:, rows - lat_width :] if lat_step < 0 else block[:, :lat_width]
    if lon_step:
        block = block[:, :, cols - lon_width :] if lon_step < 0 else block[:, :, :lon_width]
    if not lat_step:
        pairs = [(lo, (lo - lon_step) % lon_count) for lo in range(lon_count)]
        return lax.ppermute(block, "lon", pairs)
    pairs = [
        (la * lon_count + lo, (la - lat_step) * lon_count + (lo - lon_step) % lon_count)
        for la in range(lat_count)
        for lo in range(lon_count)
        if 0 <= la - lat_step < lat_count
    ]
    if not lon_step:
        pairs = [(s // lon_count, t // lon_count) for s, t in pairs if s % lon_count == 0]
        return lax.ppermute(block, "lat", pairs)
    return lax.ppermute(block, ("lat", "lon"), pairs)


def framed_of(block, extra, lat_width, lon_width):
    channels = block.shape[0]
    tall = jnp.concatenate([block, extra], axis=0)
    above = neighbour_piece(tall, -1, 0, lat_width, lon_width)
    below = neighbour_piece(tall, 1, 0, lat_width, lon_width)
    bands = []
    for lat_step, centre in ((-1, above[:channels]), (0, block), (1, below[:channels])):
        left = neighbour_piece(block, lat_step, -1, lat_width, lon_width)
        right = neighbour_piece(block, lat_step, 1, lat_width, lon_width)
        bands.append(jnp.concatenate([left, centre, right], axis=2))
    extra_rows = jnp.concatenate([above[channels:], extra, below[channels:]], axis=1)
    return jnp.concatenate(bands, axis=1), extra_rows


def coefficients(quadrature, lat_offsets, lon_offsets):
    lat_levels = jnp.arange(2 * LAT_REACH + 1, dtype=jnp.int32)
    lon_levels = jnp.arange(2 * LON_REACH + 1, dtype=jnp.int32)
    lat_onehot = (lat_offsets[..., None] + LAT_REACH == lat_levels).astype(jnp.float32)
    lon_onehot = (lon_offsets[..., None] + LON_REACH == lon_levels).astype(jnp.float32)
    stencil = jnp.einsum(
        "rks,rksa,rksd->krad", quadrature, lat_onehot, lon_onehot, precision=lax.Precision.HIGHEST
    )
    return stencil.astype(jnp.bfloat16)


def lon_picker(col_count, first_source=0, source_count=None):
    span_count = 2 * LON_REACH + 1
    if source_count is None:
        source_count = col_count + 2 * LON_REACH
    table_shape = (span_count, source_count, col_count)
    offset_level = lax.broadcasted_iota(jnp.int32, table_shape, 0)
    source = lax.broadcasted_iota(jnp.int32, table_shape, 1) + first_source
    target = lax.broadcasted_iota(jnp.int32, table_shape, 2)
    matches = source - target == offset_level
    return matches.astype(jnp.bfloat16)


def band_of(stencil, col_count, first_source=0, source_count=None):
    return jnp.einsum(
        "kiad,dpq->iapkq",
        stencil,
        lon_picker(col_count, first_source, source_count),
        preferred_element_type=jnp.float32,
    ).astype(jnp.bfloat16)


def spread(values, band, basis_count):
    row_count = values.shape[1] - 2 * LAT_REACH
    lat_taps = 2 * LAT_REACH + 1
    stacked = jnp.stack(
        [values[:, offset : offset + row_count] for offset in range(lat_taps)], axis=2
    )
    return jnp.einsum("ciap,iapkq->cikq", stacked, band, preferred_element_type=jnp.float32)


def spread_adjoint(mixed, band):
    row_count, col_count = mixed.shape[1], mixed.shape[3]
    lat_taps = 2 * LAT_REACH + 1
    partial = jnp.einsum("cikq,iapkq->ciap", mixed, band, preferred_element_type=jnp.float32)
    if partial.shape[3] != col_count - LON_HALO:
        partial = partial[:, :, :, LON_HALO : col_count]
    out_rows = row_count - LAT_HALO
    total = partial[:, LAT_HALO : LAT_HALO + out_rows, 0]
    for offset in range(1, lat_taps):
        start = LAT_HALO - offset
        total = total + partial[:, start : start + out_rows, offset]
    return total


def mix_channels(weight, spreaded):
    return jnp.einsum("koc,cikj->oij", weight, spreaded, preferred_element_type=jnp.float32)


def unmix(weight, grad_rows):
    return jnp.einsum(
        "koc,oij->cikj", weight, grad_rows, preferred_element_type=jnp.float32
    ).astype(jnp.bfloat16)


def filter_term(gradient, spreaded):
    return jnp.einsum("oij,cikj->koc", gradient, spreaded, preferred_element_type=jnp.float32)


def body(state_field, first_weight, second_weight, quadrature, lat_offsets, lon_offsets, cotangent):
    source = state_field[0]
    gradient = cotangent[0]
    channels, row_count, col_count = source.shape
    stencil = coefficients(quadrature, lat_offsets, lon_offsets)
    basis_count = stencil.shape[0]

    packed = jnp.concatenate([source, gradient], axis=0)
    taps_per_row = stencil.size // row_count
    stencil_rows = jnp.transpose(stencil, (1, 0, 2, 3)).reshape(row_count, taps_per_row)
    stencil_rows = jnp.pad(stencil_rows, ((0, 0), (0, col_count - taps_per_row)))
    framed, stencil_wide = framed_of(packed, stencil_rows[None], LAT_HALO, LON_HALO)
    source_wide, gradient_wide = framed[:channels], framed[channels:]
    stencil_wide = stencil_wide[0, :, :taps_per_row].reshape(
        row_count + 2 * LAT_HALO, stencil.shape[0], stencil.shape[2], stencil.shape[3]
    )
    stencil_wide = jnp.transpose(stencil_wide, (1, 0, 2, 3))

    total_rows = row_count * lax.axis_size("lat")
    first_row = lax.axis_index("lat") * row_count
    near_rows = first_row - LAT_REACH + jnp.arange(row_count + 2 * LAT_REACH)
    near_valid = ((near_rows >= 0) & (near_rows < total_rows))[None, :, None]

    near_band = band_of(stencil_wide[:, LAT_REACH : LAT_REACH + row_count + 2 * LAT_REACH], col_count + LON_HALO)
    own_band = band_of(stencil, col_count)
    wide_band = band_of(stencil_wide, col_count + 2 * LON_HALO, LON_HALO, col_count + LON_HALO)

    first_near = spread(source_wide, near_band, basis_count).astype(jnp.bfloat16)
    hidden = mix_channels(first_weight, first_near)
    activation = jnp.where(near_valid, jax.nn.gelu(hidden), 0.0).astype(jnp.bfloat16)
    second_spread = spread(activation, own_band, basis_count).astype(jnp.bfloat16)
    own_gradient = gradient_wide[:, LAT_HALO : LAT_HALO + row_count, LON_HALO : LON_HALO + col_count]
    second_sum = filter_term(own_gradient, second_spread)

    second_mixed = unmix(second_weight, gradient_wide)
    activation_grad = spread_adjoint(second_mixed, wide_band).astype(jnp.bfloat16)
    hidden_grad = jax.vjp(jax.nn.gelu, hidden)[1](activation_grad.astype(jnp.float32))[0]
    hidden_grad = jnp.where(near_valid, hidden_grad, 0.0).astype(jnp.bfloat16)
    own_hidden_grad = hidden_grad[:, LAT_REACH : LAT_REACH + row_count, LON_REACH : LON_REACH + col_count]
    own_first = first_near[:, LAT_REACH : LAT_REACH + row_count, :, LON_REACH : LON_REACH + col_count]
    first_sum = filter_term(own_hidden_grad, own_first)
    member_total = state_field.shape[0] * lax.axis_size("ens")
    grad_scale = 1.0 / math.sqrt(
        member_total * row_count * lax.axis_size("lat") * col_count * lax.axis_size("lon")
    )
    axes = ("ens", "lat", "lon")
    second_grad, second_spread = halving_sum(second_sum * grad_scale, axes, hold=second_spread)
    first_grad, hidden_grad = halving_sum(first_sum * grad_scale, axes, hold=hidden_grad)
    layer_output = mix_channels(second_weight, second_spread).astype(jnp.bfloat16)
    first_mixed = unmix(first_weight, hidden_grad)
    state_grad = spread_adjoint(first_mixed, near_band).astype(jnp.bfloat16)
    return (layer_output[None], state_grad[None], first_grad, second_grad)


def solution(mesh):
    in_specs = (
        P("ens", None, "lat", "lon"),
        P(),
        P(),
        P("lat", None, None),
        P("lat", None, None),
        P("lat", None, None),
        P("ens", None, "lat", "lon"),
    )
    out_specs = (P("ens", None, "lat", "lon"), P("ens", None, "lat", "lon"), P(), P())
    return jax.shard_map(body, mesh=mesh, in_specs=in_specs, out_specs=out_specs, check_vma=False)
```

```python
import math

import jax
import jax.numpy as jnp
from jax import lax
from jax.sharding import PartitionSpec as P

LAT_REACH = 1
LON_REACH = 4
LAT_HALO = 2 * LAT_REACH
LON_HALO = 2 * LON_REACH


def halving_sum(value, axes, exchanged=2, hold=None):
    stages = []
    for axis in axes:
        bit = 1
        while bit < lax.axis_size(axis):
            stages.append((axis, bit))
            bit *= 2
    exchanged = min(exchanged, len(stages))
    halved = stages[: len(stages) - exchanged]
    flat = value.reshape(-1, value.shape[-1])
    held = hold
    for axis, bit in halved:
        pairs = [(i, i ^ bit) for i in range(lax.axis_size(axis))]
        upper = (lax.axis_index(axis) // bit) % 2
        half = flat.shape[0] // 2
        keep = lax.dynamic_slice_in_dim(flat, upper * half, half)
        send = lax.dynamic_slice_in_dim(flat, (1 - upper) * half, half)
        flat = keep + lax.ppermute(send, axis, pairs)
        if hold is not None:
            flat, hold = lax.optimization_barrier((flat, hold))
            held, hold = hold, None
    for axis, bit in stages[len(halved) :]:
        pairs = [(i, i ^ bit) for i in range(lax.axis_size(axis))]
        flat = flat + lax.ppermute(flat, axis, pairs)
    flat = flat.astype(jnp.bfloat16)
    for axis, bit in reversed(halved):
        pairs = [(i, i ^ bit) for i in range(lax.axis_size(axis))]
        upper = (lax.axis_index(axis) // bit) % 2
        other = lax.ppermute(flat, axis, pairs)
        flat = jnp.where(
            upper == 1, jnp.concatenate([other, flat]), jnp.concatenate([flat, other])
        )
    return flat.astype(jnp.float32).reshape(value.shape), held


def lat_halo(block, dim, width):
    count = lax.axis_size("lat")
    rows = block.shape[dim]
    if count == 2 and width == rows:
        other = lax.ppermute(block, "lat", [(0, 1), (1, 0)])
        lower = lax.axis_index("lat") == 0
        blank = jnp.zeros_like(other)
        above = jnp.where(lower, blank, other)
        below = jnp.where(lower, other, blank)
        return jnp.concatenate([above, block, below], axis=dim)
    above = lax.ppermute(
        lax.slice_in_dim(block, rows - width, rows, axis=dim),
        "lat",
        [(i, i + 1) for i in range(count - 1)],
    )
    below = lax.ppermute(
        lax.slice_in_dim(block, 0, width, axis=dim), "lat", [(i + 1, i) for i in range(count - 1)]
    )
    return jnp.concatenate([above, block, below], axis=dim)


def lon_halo(block, width):
    count = lax.axis_size("lon")
    cols = block.shape[-1]
    left = lax.ppermute(block[..., cols - width :], "lon", [(i, (i + 1) % count) for i in range(count)])
    right = lax.ppermute(block[..., :width], "lon", [(i, (i - 1) % count) for i in range(count)])
    return jnp.concatenate([left, block, right], axis=-1)


def coefficients(quadrature, lat_offsets, lon_offsets):
    lat_levels = jnp.arange(2 * LAT_REACH + 1, dtype=jnp.int32)
    lon_levels = jnp.arange(2 * LON_REACH + 1, dtype=jnp.int32)
    lat_onehot = (lat_offsets[..., None] + LAT_REACH == lat_levels).astype(jnp.float32)
    lon_onehot = (lon_offsets[..., None] + LON_REACH == lon_levels).astype(jnp.float32)
    stencil = jnp.einsum(
        "rks,rksa,rksd->krad", quadrature, lat_onehot, lon_onehot, precision=lax.Precision.HIGHEST
    )
    return stencil.astype(jnp.bfloat16)


def lon_picker(col_count, first_source=0, source_count=None):
    span_count = 2 * LON_REACH + 1
    if source_count is None:
        source_count = col_count + 2 * LON_REACH
    table_shape = (span_count, source_count, col_count)
    offset_level = lax.broadcasted_iota(jnp.int32, table_shape, 0)
    source = lax.broadcasted_iota(jnp.int32, table_shape, 1) + first_source
    target = lax.broadcasted_iota(jnp.int32, table_shape, 2)
    matches = source - target == offset_level
    return matches.astype(jnp.bfloat16)


def band_of(stencil, col_count, first_source=0, source_count=None):
    return jnp.einsum(
        "kiad,dpq->iapkq",
        stencil,
        lon_picker(col_count, first_source, source_count),
        preferred_element_type=jnp.float32,
    ).astype(jnp.bfloat16)


def spread(values, band, basis_count):
    row_count = values.shape[1] - 2 * LAT_REACH
    lat_taps = 2 * LAT_REACH + 1
    stacked = jnp.stack(
        [values[:, offset : offset + row_count] for offset in range(lat_taps)], axis=2
    )
    return jnp.einsum("ciap,iapkq->cikq", stacked, band, preferred_element_type=jnp.float32)


def spread_adjoint(mixed, band):
    row_count, col_count = mixed.shape[1], mixed.shape[3]
    lat_taps = 2 * LAT_REACH + 1
    partial = jnp.einsum("cikq,iapkq->ciap", mixed, band, preferred_element_type=jnp.float32)
    if partial.shape[3] != col_count - LON_HALO:
        partial = partial[:, :, :, LON_HALO : col_count]
    out_rows = row_count - LAT_HALO
    total = partial[:, LAT_HALO : LAT_HALO + out_rows, 0]
    for offset in range(1, lat_taps):
        start = LAT_HALO - offset
        total = total + partial[:, start : start + out_rows, offset]
    return total


def mix_channels(weight, spreaded):
    return jnp.einsum("koc,cikj->oij", weight, spreaded, preferred_element_type=jnp.float32)


def unmix(weight, grad_rows):
    return jnp.einsum(
        "koc,oij->cikj", weight, grad_rows, preferred_element_type=jnp.float32
    ).astype(jnp.bfloat16)


def filter_term(gradient, spreaded):
    return jnp.einsum("oij,cikj->koc", gradient, spreaded, preferred_element_type=jnp.float32)


def body(state_field, first_weight, second_weight, quadrature, lat_offsets, lon_offsets, cotangent):
    source = state_field[0]
    gradient = cotangent[0]
    channels, row_count, col_count = source.shape
    stencil = coefficients(quadrature, lat_offsets, lon_offsets)
    basis_count = stencil.shape[0]

    packed = lon_halo(jnp.concatenate([source, gradient], axis=0), LON_HALO)
    taps_per_row = stencil.size // row_count
    stencil_rows = jnp.transpose(stencil, (1, 0, 2, 3)).reshape(row_count, taps_per_row)
    stencil_rows = jnp.pad(stencil_rows, ((0, 0), (0, packed.shape[2] - taps_per_row)))
    framed = lat_halo(jnp.concatenate([packed, stencil_rows[None]], axis=0), 1, LAT_HALO)
    source_wide, gradient_wide = framed[:channels], framed[channels : 2 * channels]
    stencil_wide = framed[2 * channels, :, :taps_per_row].reshape(
        row_count + 2 * LAT_HALO, stencil.shape[0], stencil.shape[2], stencil.shape[3]
    )
    stencil_wide = jnp.transpose(stencil_wide, (1, 0, 2, 3))

    total_rows = row_count * lax.axis_size("lat")
    first_row = lax.axis_index("lat") * row_count
    near_rows = first_row - LAT_REACH + jnp.arange(row_count + 2 * LAT_REACH)
    near_valid = ((near_rows >= 0) & (near_rows < total_rows))[None, :, None]

    near_band = band_of(stencil_wide[:, LAT_REACH : LAT_REACH + row_count + 2 * LAT_REACH], col_count + LON_HALO)
    own_band = band_of(stencil, col_count)
    wide_band = band_of(stencil_wide, col_count + 2 * LON_HALO, LON_HALO, col_count + LON_HALO)

    first_near = spread(source_wide, near_band, basis_count).astype(jnp.bfloat16)
    hidden = mix_channels(first_weight, first_near)
    activation = jnp.where(near_valid, jax.nn.gelu(hidden), 0.0).astype(jnp.bfloat16)
    second_spread = spread(activation, own_band, basis_count).astype(jnp.bfloat16)
    own_gradient = gradient_wide[:, LAT_HALO : LAT_HALO + row_count, LON_HALO : LON_HALO + col_count]
    second_sum = filter_term(own_gradient, second_spread)

    second_mixed = unmix(second_weight, gradient_wide)
    activation_grad = spread_adjoint(second_mixed, wide_band).astype(jnp.bfloat16)
    hidden_grad = jax.vjp(jax.nn.gelu, hidden)[1](activation_grad.astype(jnp.float32))[0]
    hidden_grad = jnp.where(near_valid, hidden_grad, 0.0).astype(jnp.bfloat16)
    own_hidden_grad = hidden_grad[:, LAT_REACH : LAT_REACH + row_count, LON_REACH : LON_REACH + col_count]
    own_first = first_near[:, LAT_REACH : LAT_REACH + row_count, :, LON_REACH : LON_REACH + col_count]
    first_sum = filter_term(own_hidden_grad, own_first)
    member_total = state_field.shape[0] * lax.axis_size("ens")
    grad_scale = 1.0 / math.sqrt(
        member_total * row_count * lax.axis_size("lat") * col_count * lax.axis_size("lon")
    )
    axes = ("ens", "lat", "lon")
    second_grad, second_spread = halving_sum(second_sum * grad_scale, axes, hold=second_spread)
    first_grad, hidden_grad = halving_sum(first_sum * grad_scale, axes, hold=hidden_grad)
    layer_output = mix_channels(second_weight, second_spread).astype(jnp.bfloat16)
    first_mixed = unmix(first_weight, hidden_grad)
    state_grad = spread_adjoint(first_mixed, near_band).astype(jnp.bfloat16)
    return (layer_output[None], state_grad[None], first_grad, second_grad)


def solution(mesh):
    in_specs = (
        P("ens", None, "lat", "lon"),
        P(),
        P(),
        P("lat", None, None),
        P("lat", None, None),
        P("lat", None, None),
        P("ens", None, "lat", "lon"),
    )
    out_specs = (P("ens", None, "lat", "lon"), P("ens", None, "lat", "lon"), P(), P())
    return jax.shard_map(body, mesh=mesh, in_specs=in_specs, out_specs=out_specs, check_vma=False)
```

```python
import math

import jax
import jax.numpy as jnp
from jax import lax
from jax.sharding import PartitionSpec as P

LAT_REACH = 1
LON_REACH = 4
LAT_HALO = 2 * LAT_REACH
LON_HALO = 2 * LON_REACH


def halving_sum(value, axes, exchanged=2, hold=None):
    stages = []
    for axis in axes:
        bit = 1
        while bit < lax.axis_size(axis):
            stages.append((axis, bit))
            bit *= 2
    exchanged = min(exchanged, len(stages))
    halved = stages[: len(stages) - exchanged]
    flat = value.reshape(-1, value.shape[-1])
    held = hold
    for axis, bit in halved:
        pairs = [(i, i ^ bit) for i in range(lax.axis_size(axis))]
        upper = (lax.axis_index(axis) // bit) % 2
        half = flat.shape[0] // 2
        keep = lax.dynamic_slice_in_dim(flat, upper * half, half)
        send = lax.dynamic_slice_in_dim(flat, (1 - upper) * half, half)
        flat = keep + lax.ppermute(send, axis, pairs)
        if hold is not None:
            flat, hold = lax.optimization_barrier((flat, hold))
            held, hold = hold, None
    for axis, bit in stages[len(halved) :]:
        pairs = [(i, i ^ bit) for i in range(lax.axis_size(axis))]
        flat = flat + lax.ppermute(flat, axis, pairs)
    flat = flat.astype(jnp.bfloat16)
    for axis, bit in reversed(halved):
        pairs = [(i, i ^ bit) for i in range(lax.axis_size(axis))]
        upper = (lax.axis_index(axis) // bit) % 2
        other = lax.ppermute(flat, axis, pairs)
        flat = jnp.where(
            upper == 1, jnp.concatenate([other, flat]), jnp.concatenate([flat, other])
        )
    return flat.astype(jnp.float32).reshape(value.shape), held


def lat_halo(block, dim, width):
    count = lax.axis_size("lat")
    rows = block.shape[dim]
    if count == 2 and width == rows:
        other = lax.ppermute(block, "lat", [(0, 1), (1, 0)])
        lower = lax.axis_index("lat") == 0
        blank = jnp.zeros_like(other)
        above = jnp.where(lower, blank, other)
        below = jnp.where(lower, other, blank)
        return jnp.concatenate([above, block, below], axis=dim)
    above = lax.ppermute(
        lax.slice_in_dim(block, rows - width, rows, axis=dim),
        "lat",
        [(i, i + 1) for i in range(count - 1)],
    )
    below = lax.ppermute(
        lax.slice_in_dim(block, 0, width, axis=dim), "lat", [(i + 1, i) for i in range(count - 1)]
    )
    return jnp.concatenate([above, block, below], axis=dim)


def lon_halo(block, width):
    count = lax.axis_size("lon")
    cols = block.shape[-1]
    left = lax.ppermute(block[..., cols - width :], "lon", [(i, (i + 1) % count) for i in range(count)])
    right = lax.ppermute(block[..., :width], "lon", [(i, (i - 1) % count) for i in range(count)])
    return jnp.concatenate([left, block, right], axis=-1)


def coefficients(quadrature, lat_offsets, lon_offsets):
    lat_levels = jnp.arange(2 * LAT_REACH + 1, dtype=jnp.int32)
    lon_levels = jnp.arange(2 * LON_REACH + 1, dtype=jnp.int32)
    lat_onehot = (lat_offsets[..., None] + LAT_REACH == lat_levels).astype(jnp.float32)
    lon_onehot = (lon_offsets[..., None] + LON_REACH == lon_levels).astype(jnp.float32)
    stencil = jnp.einsum(
        "rks,rksa,rksd->krad", quadrature, lat_onehot, lon_onehot, precision=lax.Precision.HIGHEST
    )
    return stencil.astype(jnp.bfloat16)


def lon_picker(col_count, first_source=0, source_count=None):
    span_count = 2 * LON_REACH + 1
    if source_count is None:
        source_count = col_count + 2 * LON_REACH
    table_shape = (span_count, source_count, col_count)
    offset_level = lax.broadcasted_iota(jnp.int32, table_shape, 0)
    source = lax.broadcasted_iota(jnp.int32, table_shape, 1) + first_source
    target = lax.broadcasted_iota(jnp.int32, table_shape, 2)
    matches = source - target == offset_level
    return matches.astype(jnp.bfloat16)


def band_of(stencil, col_count, first_source=0, source_count=None):
    return jnp.einsum(
        "kiad,dpq->iapkq",
        stencil,
        lon_picker(col_count, first_source, source_count),
        preferred_element_type=jnp.float32,
    ).astype(jnp.bfloat16)


def spread(values, band, basis_count):
    row_count = values.shape[1] - 2 * LAT_REACH
    lat_taps = 2 * LAT_REACH + 1
    stacked = jnp.stack(
        [values[:, offset : offset + row_count] for offset in range(lat_taps)], axis=2
    )
    return jnp.einsum("ciap,iapkq->cikq", stacked, band, preferred_element_type=jnp.float32)


def spread_adjoint(mixed, band):
    row_count, col_count = mixed.shape[1], mixed.shape[3]
    lat_taps = 2 * LAT_REACH + 1
    partial = jnp.einsum("cikq,iapkq->ciap", mixed, band, preferred_element_type=jnp.float32)
    if partial.shape[3] != col_count - LON_HALO:
        partial = partial[:, :, :, LON_HALO : col_count]
    out_rows = row_count - LAT_HALO
    total = partial[:, LAT_HALO : LAT_HALO + out_rows, 0]
    for offset in range(1, lat_taps):
        start = LAT_HALO - offset
        total = total + partial[:, start : start + out_rows, offset]
    return total


def spread_adjoint_rows(mixed, band):
    col_count = mixed.shape[3]
    partial = jnp.einsum("cikq,iapkq->ciap", mixed, band, preferred_element_type=jnp.float32)
    if partial.shape[3] != col_count - LON_HALO:
        partial = partial[:, :, :, LON_HALO : col_count]
    below = jnp.pad(partial[:, 1:, 0], ((0, 0), (0, 1), (0, 0)))
    above = jnp.pad(partial[:, :-1, 2], ((0, 0), (1, 0), (0, 0)))
    return partial[:, :, 1] + below + above


def mix_channels(weight, spreaded):
    return jnp.einsum("koc,cikj->oij", weight, spreaded, preferred_element_type=jnp.float32)


def unmix(weight, grad_rows):
    return jnp.einsum(
        "koc,oij->cikj", weight, grad_rows, preferred_element_type=jnp.float32
    ).astype(jnp.bfloat16)


def filter_term(gradient, spreaded):
    return jnp.einsum("oij,cikj->koc", gradient, spreaded, preferred_element_type=jnp.float32)


def body(state_field, first_weight, second_weight, quadrature, lat_offsets, lon_offsets, cotangent):
    source = state_field[0]
    gradient = cotangent[0]
    channels, row_count, col_count = source.shape
    stencil = coefficients(quadrature, lat_offsets, lon_offsets)
    basis_count = stencil.shape[0]

    packed = lon_halo(jnp.concatenate([source, gradient], axis=0), LON_HALO)
    taps_per_row = stencil.size // row_count
    stencil_rows = jnp.transpose(stencil, (1, 0, 2, 3)).reshape(row_count, taps_per_row)
    stencil_rows = jnp.pad(stencil_rows, ((0, 0), (0, packed.shape[2] - taps_per_row)))
    framed = lat_halo(jnp.concatenate([packed, stencil_rows[None]], axis=0), 1, LAT_HALO)
    source_wide, gradient_wide = framed[:channels], framed[channels : 2 * channels]
    stencil_wide = framed[2 * channels, :, :taps_per_row].reshape(
        row_count + 2 * LAT_HALO, stencil.shape[0], stencil.shape[2], stencil.shape[3]
    )
    stencil_wide = jnp.transpose(stencil_wide, (1, 0, 2, 3))

    total_rows = row_count * lax.axis_size("lat")
    first_row = lax.axis_index("lat") * row_count
    near_rows = first_row - LAT_REACH + jnp.arange(row_count + 2 * LAT_REACH)
    near_valid = ((near_rows >= 0) & (near_rows < total_rows))[None, :, None]

    near_band = band_of(stencil_wide[:, LAT_REACH : LAT_REACH + row_count + 2 * LAT_REACH], col_count + LON_HALO)
    own_band = band_of(stencil, col_count)
    wide_band = band_of(stencil_wide, col_count + 2 * LON_HALO, LON_HALO, col_count + LON_HALO)

    first_near = spread(source_wide, near_band, basis_count).astype(jnp.bfloat16)
    hidden = mix_channels(first_weight, first_near)
    activation = jnp.where(near_valid, jax.nn.gelu(hidden), 0.0).astype(jnp.bfloat16)
    second_spread = spread(activation, own_band, basis_count).astype(jnp.bfloat16)
    own_gradient = gradient_wide[:, LAT_HALO : LAT_HALO + row_count, LON_HALO : LON_HALO + col_count]
    second_sum = filter_term(own_gradient, second_spread)

    if lax.axis_size("lat") == 2 and row_count == LAT_HALO:
        lower = lax.axis_index("lat") == 0
        grid_gradient = jnp.where(lower, gradient_wide[:, row_count:], gradient_wide[:, : 2 * row_count])
        grid_stencil = jnp.where(lower, stencil_wide[:, row_count:], stencil_wide[:, : 2 * row_count])
        grid_band = band_of(grid_stencil, col_count + 2 * LON_HALO, LON_HALO, col_count + LON_HALO)
        second_mixed = unmix(second_weight, grid_gradient)
        grid_grad = spread_adjoint_rows(second_mixed, grid_band).astype(jnp.bfloat16)
        edge = jnp.zeros_like(grid_grad[:, :LAT_REACH])
        activation_grad = jnp.where(
            lower,
            jnp.concatenate([edge, grid_grad[:, : 2 * row_count - LAT_REACH]], axis=1),
            jnp.concatenate([grid_grad[:, LAT_REACH:], edge], axis=1),
        )
    else:
        second_mixed = unmix(second_weight, gradient_wide)
        activation_grad = spread_adjoint(second_mixed, wide_band).astype(jnp.bfloat16)
    hidden_grad = jax.vjp(jax.nn.gelu, hidden)[1](activation_grad.astype(jnp.float32))[0]
    hidden_grad = jnp.where(near_valid, hidden_grad, 0.0).astype(jnp.bfloat16)
    own_hidden_grad = hidden_grad[:, LAT_REACH : LAT_REACH + row_count, LON_REACH : LON_REACH + col_count]
    own_first = first_near[:, LAT_REACH : LAT_REACH + row_count, :, LON_REACH : LON_REACH + col_count]
    first_sum = filter_term(own_hidden_grad, own_first)
    member_total = state_field.shape[0] * lax.axis_size("ens")
    grad_scale = 1.0 / math.sqrt(
        member_total * row_count * lax.axis_size("lat") * col_count * lax.axis_size("lon")
    )
    axes = ("ens", "lat", "lon")
    second_grad, second_spread = halving_sum(second_sum * grad_scale, axes, hold=second_spread)
    first_grad, hidden_grad = halving_sum(first_sum * grad_scale, axes, hold=hidden_grad)
    layer_output = mix_channels(second_weight, second_spread).astype(jnp.bfloat16)
    first_mixed = unmix(first_weight, hidden_grad)
    state_grad = spread_adjoint(first_mixed, near_band).astype(jnp.bfloat16)
    return (layer_output[None], state_grad[None], first_grad, second_grad)


def solution(mesh):
    in_specs = (
        P("ens", None, "lat", "lon"),
        P(),
        P(),
        P("lat", None, None),
        P("lat", None, None),
        P("lat", None, None),
        P("ens", None, "lat", "lon"),
    )
    out_specs = (P("ens", None, "lat", "lon"), P("ens", None, "lat", "lon"), P(), P())
    return jax.shard_map(body, mesh=mesh, in_specs=in_specs, out_specs=out_specs, check_vma=False)
```

```python
import math

import jax
import jax.numpy as jnp
from jax import lax
from jax.sharding import PartitionSpec as P

LAT_REACH = 1
LON_REACH = 4
LAT_HALO = 2 * LAT_REACH
LON_HALO = 2 * LON_REACH


def halving_sum(value, axes, exchanged=2, hold=None):
    stages = []
    for axis in axes:
        bit = 1
        while bit < lax.axis_size(axis):
            stages.append((axis, bit))
            bit *= 2
    exchanged = min(exchanged, len(stages))
    halved = stages[: len(stages) - exchanged]
    flat = value.reshape(-1, value.shape[-1])
    held = hold
    for axis, bit in halved:
        pairs = [(i, i ^ bit) for i in range(lax.axis_size(axis))]
        upper = (lax.axis_index(axis) // bit) % 2
        half = flat.shape[0] // 2
        keep = lax.dynamic_slice_in_dim(flat, upper * half, half)
        send = lax.dynamic_slice_in_dim(flat, (1 - upper) * half, half)
        flat = keep + lax.ppermute(send, axis, pairs)
        if hold is not None:
            flat, hold = lax.optimization_barrier((flat, hold))
            held, hold = hold, None
    for axis, bit in stages[len(halved) :]:
        pairs = [(i, i ^ bit) for i in range(lax.axis_size(axis))]
        flat = flat + lax.ppermute(flat, axis, pairs)
    flat = flat.astype(jnp.bfloat16)
    for step, (axis, bit) in enumerate(reversed(halved)):
        pairs = [(i, i ^ bit) for i in range(lax.axis_size(axis))]
        upper = (lax.axis_index(axis) // bit) % 2
        other = lax.ppermute(flat, axis, pairs)
        if step == len(halved) - 1:
            flat, other = flat.astype(jnp.float32), other.astype(jnp.float32)
        flat = jnp.where(
            upper == 1, jnp.concatenate([other, flat]), jnp.concatenate([flat, other])
        )
    return flat.astype(jnp.float32).reshape(value.shape), held


def lat_halo(block, dim, width):
    count = lax.axis_size("lat")
    rows = block.shape[dim]
    if count == 2 and width == rows:
        other = lax.ppermute(block, "lat", [(0, 1), (1, 0)])
        lower = lax.axis_index("lat") == 0
        blank = jnp.zeros_like(other)
        above = jnp.where(lower, blank, other)
        below = jnp.where(lower, other, blank)
        return jnp.concatenate([above, block, below], axis=dim)
    above = lax.ppermute(
        lax.slice_in_dim(block, rows - width, rows, axis=dim),
        "lat",
        [(i, i + 1) for i in range(count - 1)],
    )
    below = lax.ppermute(
        lax.slice_in_dim(block, 0, width, axis=dim), "lat", [(i + 1, i) for i in range(count - 1)]
    )
    return jnp.concatenate([above, block, below], axis=dim)


def lon_halo(block, width):
    count = lax.axis_size("lon")
    cols = block.shape[-1]
    left = lax.ppermute(block[..., cols - width :], "lon", [(i, (i + 1) % count) for i in range(count)])
    right = lax.ppermute(block[..., :width], "lon", [(i, (i - 1) % count) for i in range(count)])
    return jnp.concatenate([left, block, right], axis=-1)


def coefficients(quadrature, lat_offsets, lon_offsets):
    lat_levels = jnp.arange(2 * LAT_REACH + 1, dtype=jnp.int32)
    lon_levels = jnp.arange(2 * LON_REACH + 1, dtype=jnp.int32)
    lat_onehot = (lat_offsets[..., None] + LAT_REACH == lat_levels).astype(jnp.float32)
    lon_onehot = (lon_offsets[..., None] + LON_REACH == lon_levels).astype(jnp.float32)
    stencil = jnp.einsum(
        "rks,rksa,rksd->krad", quadrature, lat_onehot, lon_onehot, precision=lax.Precision.HIGHEST
    )
    return stencil.astype(jnp.bfloat16)


def lon_picker(col_count, first_source=0, source_count=None):
    span_count = 2 * LON_REACH + 1
    if source_count is None:
        source_count = col_count + 2 * LON_REACH
    table_shape = (span_count, source_count, col_count)
    offset_level = lax.broadcasted_iota(jnp.int32, table_shape, 0)
    source = lax.broadcasted_iota(jnp.int32, table_shape, 1) + first_source
    target = lax.broadcasted_iota(jnp.int32, table_shape, 2)
    matches = source - target == offset_level
    return matches.astype(jnp.bfloat16)


def band_of(stencil, col_count, first_source=0, source_count=None):
    return jnp.einsum(
        "kiad,dpq->iapkq",
        stencil,
        lon_picker(col_count, first_source, source_count),
        preferred_element_type=jnp.float32,
    ).astype(jnp.bfloat16)


def spread(values, band, basis_count):
    row_count = values.shape[1] - 2 * LAT_REACH
    lat_taps = 2 * LAT_REACH + 1
    stacked = jnp.stack(
        [values[:, offset : offset + row_count] for offset in range(lat_taps)], axis=2
    )
    return jnp.einsum("ciap,iapkq->cikq", stacked, band, preferred_element_type=jnp.float32)


def spread_adjoint(mixed, band):
    row_count, col_count = mixed.shape[1], mixed.shape[3]
    lat_taps = 2 * LAT_REACH + 1
    partial = jnp.einsum("cikq,iapkq->ciap", mixed, band, preferred_element_type=jnp.float32)
    if partial.shape[3] != col_count - LON_HALO:
        partial = partial[:, :, :, LON_HALO : col_count]
    out_rows = row_count - LAT_HALO
    total = partial[:, LAT_HALO : LAT_HALO + out_rows, 0]
    for offset in range(1, lat_taps):
        start = LAT_HALO - offset
        total = total + partial[:, start : start + out_rows, offset]
    return total


def spread_adjoint_rows(mixed, band):
    col_count = mixed.shape[3]
    partial = jnp.einsum("cikq,iapkq->ciap", mixed, band, preferred_element_type=jnp.float32)
    if partial.shape[3] != col_count - LON_HALO:
        partial = partial[:, :, :, LON_HALO : col_count]
    below = jnp.pad(partial[:, 1:, 0], ((0, 0), (0, 1), (0, 0)))
    above = jnp.pad(partial[:, :-1, 2], ((0, 0), (1, 0), (0, 0)))
    return partial[:, :, 1] + below + above


def mix_channels(weight, spreaded):
    return jnp.einsum("koc,cikj->oij", weight, spreaded, preferred_element_type=jnp.float32)


def unmix(weight, grad_rows):
    return jnp.einsum(
        "koc,oij->cikj", weight, grad_rows, preferred_element_type=jnp.float32
    ).astype(jnp.bfloat16)


def filter_term(gradient, spreaded):
    return jnp.einsum("oij,cikj->koc", gradient, spreaded, preferred_element_type=jnp.float32)


def body(state_field, first_weight, second_weight, quadrature, lat_offsets, lon_offsets, cotangent):
    source = state_field[0]
    gradient = cotangent[0]
    channels, row_count, col_count = source.shape
    stencil = coefficients(quadrature, lat_offsets, lon_offsets)
    basis_count = stencil.shape[0]

    packed = lon_halo(jnp.concatenate([source, gradient], axis=0), LON_HALO)
    taps_per_row = stencil.size // row_count
    stencil_rows = jnp.transpose(stencil, (1, 0, 2, 3)).reshape(row_count, taps_per_row)
    stencil_rows = jnp.pad(stencil_rows, ((0, 0), (0, packed.shape[2] - taps_per_row)))
    framed = lat_halo(jnp.concatenate([packed, stencil_rows[None]], axis=0), 1, LAT_HALO)
    source_wide, gradient_wide = framed[:channels], framed[channels : 2 * channels]
    stencil_wide = framed[2 * channels, :, :taps_per_row].reshape(
        row_count + 2 * LAT_HALO, stencil.shape[0], stencil.shape[2], stencil.shape[3]
    )
    stencil_wide = jnp.transpose(stencil_wide, (1, 0, 2, 3))

    total_rows = row_count * lax.axis_size("lat")
    first_row = lax.axis_index("lat") * row_count
    near_rows = first_row - LAT_REACH + jnp.arange(row_count + 2 * LAT_REACH)
    near_valid = ((near_rows >= 0) & (near_rows < total_rows))[None, :, None]

    near_band = band_of(stencil_wide[:, LAT_REACH : LAT_REACH + row_count + 2 * LAT_REACH], col_count + LON_HALO)
    own_band = band_of(stencil, col_count)
    wide_band = band_of(stencil_wide, col_count + 2 * LON_HALO, LON_HALO, col_count + LON_HALO)

    first_near = spread(source_wide, near_band, basis_count).astype(jnp.bfloat16)
    hidden = mix_channels(first_weight, first_near)
    activation = jnp.where(near_valid, jax.nn.gelu(hidden), 0.0).astype(jnp.bfloat16)
    second_spread = spread(activation, own_band, basis_count).astype(jnp.bfloat16)
    own_gradient = gradient_wide[:, LAT_HALO : LAT_HALO + row_count, LON_HALO : LON_HALO + col_count]
    second_sum = filter_term(own_gradient, second_spread)

    if lax.axis_size("lat") == 2 and row_count == LAT_HALO:
        lower = lax.axis_index("lat") == 0
        grid_gradient = jnp.where(lower, gradient_wide[:, row_count:], gradient_wide[:, : 2 * row_count])
        grid_stencil = jnp.where(lower, stencil_wide[:, row_count:], stencil_wide[:, : 2 * row_count])
        grid_band = band_of(grid_stencil, col_count + 2 * LON_HALO, LON_HALO, col_count + LON_HALO)
        second_mixed = unmix(second_weight, grid_gradient)
        grid_grad = spread_adjoint_rows(second_mixed, grid_band).astype(jnp.bfloat16)
        edge = jnp.zeros_like(grid_grad[:, :LAT_REACH])
        activation_grad = jnp.where(
            lower,
            jnp.concatenate([edge, grid_grad[:, : 2 * row_count - LAT_REACH]], axis=1),
            jnp.concatenate([grid_grad[:, LAT_REACH:], edge], axis=1),
        )
    else:
        second_mixed = unmix(second_weight, gradient_wide)
        activation_grad = spread_adjoint(second_mixed, wide_band).astype(jnp.bfloat16)
    hidden_grad = jax.vjp(jax.nn.gelu, hidden)[1](activation_grad.astype(jnp.float32))[0]
    hidden_grad = jnp.where(near_valid, hidden_grad, 0.0).astype(jnp.bfloat16)
    own_hidden_grad = hidden_grad[:, LAT_REACH : LAT_REACH + row_count, LON_REACH : LON_REACH + col_count]
    own_first = first_near[:, LAT_REACH : LAT_REACH + row_count, :, LON_REACH : LON_REACH + col_count]
    first_sum = filter_term(own_hidden_grad, own_first)
    member_total = state_field.shape[0] * lax.axis_size("ens")
    grad_scale = 1.0 / math.sqrt(
        member_total * row_count * lax.axis_size("lat") * col_count * lax.axis_size("lon")
    )
    axes = ("ens", "lat", "lon")
    second_grad, second_spread = halving_sum(second_sum * grad_scale, axes, hold=second_spread)
    first_grad, hidden_grad = halving_sum(first_sum * grad_scale, axes, hold=hidden_grad)
    layer_output = mix_channels(second_weight, second_spread).astype(jnp.bfloat16)
    first_mixed = unmix(first_weight, hidden_grad)
    state_grad = spread_adjoint(first_mixed, near_band).astype(jnp.bfloat16)
    return (layer_output[None], state_grad[None], first_grad, second_grad)


def solution(mesh):
    in_specs = (
        P("ens", None, "lat", "lon"),
        P(),
        P(),
        P("lat", None, None),
        P("lat", None, None),
        P("lat", None, None),
        P("ens", None, "lat", "lon"),
    )
    out_specs = (P("ens", None, "lat", "lon"), P("ens", None, "lat", "lon"), P(), P())
    return jax.shard_map(body, mesh=mesh, in_specs=in_specs, out_specs=out_specs, check_vma=False)
```

```python
import math

import jax
import jax.numpy as jnp
from jax import lax
from jax.sharding import PartitionSpec as P

LAT_REACH = 1
LON_REACH = 4
LAT_HALO = 2 * LAT_REACH
LON_HALO = 2 * LON_REACH


def halving_sum(value, axes, exchanged=2, hold=None):
    stages = []
    for axis in axes:
        bit = 1
        while bit < lax.axis_size(axis):
            stages.append((axis, bit))
            bit *= 2
    exchanged = min(exchanged, len(stages))
    halved = stages[: len(stages) - exchanged]
    flat = value.reshape(-1, value.shape[-1])
    held = hold
    for axis, bit in halved:
        pairs = [(i, i ^ bit) for i in range(lax.axis_size(axis))]
        upper = (lax.axis_index(axis) // bit) % 2
        half = flat.shape[0] // 2
        keep = lax.dynamic_slice_in_dim(flat, upper * half, half)
        send = lax.dynamic_slice_in_dim(flat, (1 - upper) * half, half)
        flat = keep + lax.ppermute(send, axis, pairs)
        if hold is not None:
            flat, hold = lax.optimization_barrier((flat, hold))
            held, hold = hold, None
    for axis, bit in stages[len(halved) :]:
        pairs = [(i, i ^ bit) for i in range(lax.axis_size(axis))]
        flat = flat + lax.ppermute(flat, axis, pairs)
    flat = flat.astype(jnp.bfloat16)
    for step, (axis, bit) in enumerate(reversed(halved)):
        pairs = [(i, i ^ bit) for i in range(lax.axis_size(axis))]
        upper = (lax.axis_index(axis) // bit) % 2
        other = lax.ppermute(flat, axis, pairs)
        if step == len(halved) - 1:
            flat, other = flat.astype(jnp.float32), other.astype(jnp.float32)
        flat = jnp.where(
            upper == 1, jnp.concatenate([other, flat]), jnp.concatenate([flat, other])
        )
    return flat.astype(jnp.float32).reshape(value.shape), held


def lat_halo(block, dim, width):
    count = lax.axis_size("lat")
    rows = block.shape[dim]
    if count == 2 and width == rows:
        other = lax.ppermute(block, "lat", [(0, 1), (1, 0)])
        lower = lax.axis_index("lat") == 0
        blank = jnp.zeros_like(other)
        above = jnp.where(lower, blank, other)
        below = jnp.where(lower, other, blank)
        return jnp.concatenate([above, block, below], axis=dim)
    above = lax.ppermute(
        lax.slice_in_dim(block, rows - width, rows, axis=dim),
        "lat",
        [(i, i + 1) for i in range(count - 1)],
    )
    below = lax.ppermute(
        lax.slice_in_dim(block, 0, width, axis=dim), "lat", [(i + 1, i) for i in range(count - 1)]
    )
    return jnp.concatenate([above, block, below], axis=dim)


def lon_halo(block, width):
    count = lax.axis_size("lon")
    cols = block.shape[-1]
    left = lax.ppermute(block[..., cols - width :], "lon", [(i, (i + 1) % count) for i in range(count)])
    right = lax.ppermute(block[..., :width], "lon", [(i, (i - 1) % count) for i in range(count)])
    return jnp.concatenate([left, block, right], axis=-1)


def coefficients(quadrature, lat_offsets, lon_offsets):
    lat_levels = jnp.arange(2 * LAT_REACH + 1, dtype=jnp.int32)
    lon_levels = jnp.arange(2 * LON_REACH + 1, dtype=jnp.int32)
    lat_onehot = (lat_offsets[..., None] + LAT_REACH == lat_levels).astype(jnp.float32)
    lon_onehot = (lon_offsets[..., None] + LON_REACH == lon_levels).astype(jnp.float32)
    stencil = jnp.einsum(
        "rks,rksa,rksd->krad", quadrature, lat_onehot, lon_onehot, precision=lax.Precision.HIGHEST
    )
    return stencil.astype(jnp.bfloat16)


def lon_picker(col_count, first_source=0, source_count=None):
    span_count = 2 * LON_REACH + 1
    if source_count is None:
        source_count = col_count + 2 * LON_REACH
    table_shape = (span_count, source_count, col_count)
    offset_level = lax.broadcasted_iota(jnp.int32, table_shape, 0)
    source = lax.broadcasted_iota(jnp.int32, table_shape, 1) + first_source
    target = lax.broadcasted_iota(jnp.int32, table_shape, 2)
    matches = source - target == offset_level
    return matches.astype(jnp.bfloat16)


def band_of(stencil, col_count, first_source=0, source_count=None):
    return jnp.einsum(
        "kiad,dpq->iapkq",
        stencil,
        lon_picker(col_count, first_source, source_count),
        preferred_element_type=jnp.float32,
    ).astype(jnp.bfloat16)


def spread(values, band, basis_count):
    row_count = values.shape[1] - 2 * LAT_REACH
    lat_taps = 2 * LAT_REACH + 1
    stacked = jnp.stack(
        [values[:, offset : offset + row_count] for offset in range(lat_taps)], axis=2
    )
    return jnp.einsum("ciap,iapkq->cikq", stacked, band, preferred_element_type=jnp.float32)


def spread_adjoint(mixed, band):
    row_count, col_count = mixed.shape[1], mixed.shape[3]
    lat_taps = 2 * LAT_REACH + 1
    partial = jnp.einsum("cikq,iapkq->ciap", mixed, band, preferred_element_type=jnp.float32)
    if partial.shape[3] != col_count - LON_HALO:
        partial = partial[:, :, :, LON_HALO : col_count]
    out_rows = row_count - LAT_HALO
    total = partial[:, LAT_HALO : LAT_HALO + out_rows, 0]
    for offset in range(1, lat_taps):
        start = LAT_HALO - offset
        total = total + partial[:, start : start + out_rows, offset]
    return total


def spread_adjoint_rows(mixed, band):
    col_count = mixed.shape[3]
    partial = jnp.einsum("cikq,iapkq->ciap", mixed, band, preferred_element_type=jnp.float32)
    if partial.shape[3] != col_count - LON_HALO:
        partial = partial[:, :, :, LON_HALO : col_count]
    below = jnp.pad(partial[:, 1:, 0], ((0, 0), (0, 1), (0, 0)))
    above = jnp.pad(partial[:, :-1, 2], ((0, 0), (1, 0), (0, 0)))
    return partial[:, :, 1] + below + above


def mix_channels(weight, spreaded):
    return jnp.einsum("koc,cikj->oij", weight, spreaded, preferred_element_type=jnp.float32)


def unmix(weight, grad_rows):
    return jnp.einsum(
        "koc,oij->cikj", weight, grad_rows, preferred_element_type=jnp.float32
    ).astype(jnp.bfloat16)


def filter_term(gradient, spreaded):
    return jnp.einsum("oij,cikj->koc", gradient, spreaded, preferred_element_type=jnp.float32)


def body(state_field, first_weight, second_weight, quadrature, lat_offsets, lon_offsets, cotangent):
    source = state_field[0]
    gradient = cotangent[0]
    channels, row_count, col_count = source.shape
    stencil = coefficients(quadrature, lat_offsets, lon_offsets)
    basis_count = stencil.shape[0]

    stencil_wide = lat_halo(stencil, 1, LAT_HALO)
    packed = lon_halo(jnp.concatenate([source, gradient], axis=0), LON_HALO)
    framed = lat_halo(packed, 1, LAT_HALO)
    source_wide, gradient_wide = framed[:channels], framed[channels:]

    total_rows = row_count * lax.axis_size("lat")
    first_row = lax.axis_index("lat") * row_count
    near_rows = first_row - LAT_REACH + jnp.arange(row_count + 2 * LAT_REACH)
    near_valid = ((near_rows >= 0) & (near_rows < total_rows))[None, :, None]

    near_band = band_of(stencil_wide[:, LAT_REACH : LAT_REACH + row_count + 2 * LAT_REACH], col_count + LON_HALO)
    own_band = band_of(stencil, col_count)
    wide_band = band_of(stencil_wide, col_count + 2 * LON_HALO, LON_HALO, col_count + LON_HALO)

    first_near = spread(source_wide, near_band, basis_count).astype(jnp.bfloat16)
    hidden = mix_channels(first_weight, first_near)
    activation = jnp.where(near_valid, jax.nn.gelu(hidden), 0.0).astype(jnp.bfloat16)
    second_spread = spread(activation, own_band, basis_count).astype(jnp.bfloat16)
    own_gradient = gradient_wide[:, LAT_HALO : LAT_HALO + row_count, LON_HALO : LON_HALO + col_count]
    second_sum = filter_term(own_gradient, second_spread)

    if lax.axis_size("lat") == 2 and row_count == LAT_HALO:
        lower = lax.axis_index("lat") == 0
        grid_gradient = jnp.where(lower, gradient_wide[:, row_count:], gradient_wide[:, : 2 * row_count])
        grid_stencil = jnp.where(lower, stencil_wide[:, row_count:], stencil_wide[:, : 2 * row_count])
        grid_band = band_of(grid_stencil, col_count + 2 * LON_HALO, LON_HALO, col_count + LON_HALO)
        second_mixed = unmix(second_weight, grid_gradient)
        grid_grad = spread_adjoint_rows(second_mixed, grid_band).astype(jnp.bfloat16)
        edge = jnp.zeros_like(grid_grad[:, :LAT_REACH])
        activation_grad = jnp.where(
            lower,
            jnp.concatenate([edge, grid_grad[:, : 2 * row_count - LAT_REACH]], axis=1),
            jnp.concatenate([grid_grad[:, LAT_REACH:], edge], axis=1),
        )
    else:
        second_mixed = unmix(second_weight, gradient_wide)
        activation_grad = spread_adjoint(second_mixed, wide_band).astype(jnp.bfloat16)
    hidden_grad = jax.vjp(jax.nn.gelu, hidden)[1](activation_grad.astype(jnp.float32))[0]
    hidden_grad = jnp.where(near_valid, hidden_grad, 0.0).astype(jnp.bfloat16)
    own_hidden_grad = hidden_grad[:, LAT_REACH : LAT_REACH + row_count, LON_REACH : LON_REACH + col_count]
    own_first = first_near[:, LAT_REACH : LAT_REACH + row_count, :, LON_REACH : LON_REACH + col_count]
    first_sum = filter_term(own_hidden_grad, own_first)
    member_total = state_field.shape[0] * lax.axis_size("ens")
    grad_scale = 1.0 / math.sqrt(
        member_total * row_count * lax.axis_size("lat") * col_count * lax.axis_size("lon")
    )
    axes = ("ens", "lat", "lon")
    second_grad, second_spread = halving_sum(second_sum * grad_scale, axes, hold=second_spread)
    first_grad, hidden_grad = halving_sum(first_sum * grad_scale, axes, hold=hidden_grad)
    layer_output = mix_channels(second_weight, second_spread).astype(jnp.bfloat16)
    first_mixed = unmix(first_weight, hidden_grad)
    state_grad = spread_adjoint(first_mixed, near_band).astype(jnp.bfloat16)
    return (layer_output[None], state_grad[None], first_grad, second_grad)


def solution(mesh):
    in_specs = (
        P("ens", None, "lat", "lon"),
        P(),
        P(),
        P("lat", None, None),
        P("lat", None, None),
        P("lat", None, None),
        P("ens", None, "lat", "lon"),
    )
    out_specs = (P("ens", None, "lat", "lon"), P("ens", None, "lat", "lon"), P(), P())
    return jax.shard_map(body, mesh=mesh, in_specs=in_specs, out_specs=out_specs, check_vma=False)
```

```python
import math

import jax
import jax.numpy as jnp
from jax import lax
from jax.sharding import PartitionSpec as P

LAT_REACH = 1
LON_REACH = 4
LAT_HALO = 2 * LAT_REACH
LON_HALO = 2 * LON_REACH


def halving_sum(value, axes, exchanged=3, hold=None):
    stages = []
    for axis in axes:
        bit = 1
        while bit < lax.axis_size(axis):
            stages.append((axis, bit))
            bit *= 2
    exchanged = min(exchanged, len(stages))
    halved = stages[: len(stages) - exchanged]
    flat = value.reshape(-1, value.shape[-1])
    held = hold
    for axis, bit in halved:
        pairs = [(i, i ^ bit) for i in range(lax.axis_size(axis))]
        upper = (lax.axis_index(axis) // bit) % 2
        half = flat.shape[0] // 2
        keep = lax.dynamic_slice_in_dim(flat, upper * half, half)
        send = lax.dynamic_slice_in_dim(flat, (1 - upper) * half, half)
        flat = keep + lax.ppermute(send, axis, pairs)
        if hold is not None:
            flat, hold = lax.optimization_barrier((flat, hold))
            held, hold = hold, None
    for axis, bit in stages[len(halved) :]:
        pairs = [(i, i ^ bit) for i in range(lax.axis_size(axis))]
        flat = flat + lax.ppermute(flat, axis, pairs)
    flat = flat.astype(jnp.bfloat16)
    for step, (axis, bit) in enumerate(reversed(halved)):
        pairs = [(i, i ^ bit) for i in range(lax.axis_size(axis))]
        upper = (lax.axis_index(axis) // bit) % 2
        other = lax.ppermute(flat, axis, pairs)
        if step == len(halved) - 1:
            flat, other = flat.astype(jnp.float32), other.astype(jnp.float32)
        flat = jnp.where(
            upper == 1, jnp.concatenate([other, flat]), jnp.concatenate([flat, other])
        )
    return flat.astype(jnp.float32).reshape(value.shape), held


def lat_halo(block, dim, width):
    count = lax.axis_size("lat")
    rows = block.shape[dim]
    if count == 2 and width == rows:
        other = lax.ppermute(block, "lat", [(0, 1), (1, 0)])
        lower = lax.axis_index("lat") == 0
        blank = jnp.zeros_like(other)
        above = jnp.where(lower, blank, other)
        below = jnp.where(lower, other, blank)
        return jnp.concatenate([above, block, below], axis=dim)
    above = lax.ppermute(
        lax.slice_in_dim(block, rows - width, rows, axis=dim),
        "lat",
        [(i, i + 1) for i in range(count - 1)],
    )
    below = lax.ppermute(
        lax.slice_in_dim(block, 0, width, axis=dim), "lat", [(i + 1, i) for i in range(count - 1)]
    )
    return jnp.concatenate([above, block, below], axis=dim)


def lon_halo(block, width):
    count = lax.axis_size("lon")
    cols = block.shape[-1]
    left = lax.ppermute(block[..., cols - width :], "lon", [(i, (i + 1) % count) for i in range(count)])
    right = lax.ppermute(block[..., :width], "lon", [(i, (i - 1) % count) for i in range(count)])
    return jnp.concatenate([left, block, right], axis=-1)


def coefficients(quadrature, lat_offsets, lon_offsets):
    lat_levels = jnp.arange(2 * LAT_REACH + 1, dtype=jnp.int32)
    lon_levels = jnp.arange(2 * LON_REACH + 1, dtype=jnp.int32)
    lat_onehot = (lat_offsets[..., None] + LAT_REACH == lat_levels).astype(jnp.float32)
    lon_onehot = (lon_offsets[..., None] + LON_REACH == lon_levels).astype(jnp.float32)
    stencil = jnp.einsum(
        "rks,rksa,rksd->krad", quadrature, lat_onehot, lon_onehot, precision=lax.Precision.HIGHEST
    )
    return stencil.astype(jnp.bfloat16)


def lon_picker(col_count, first_source=0, source_count=None):
    span_count = 2 * LON_REACH + 1
    if source_count is None:
        source_count = col_count + 2 * LON_REACH
    table_shape = (span_count, source_count, col_count)
    offset_level = lax.broadcasted_iota(jnp.int32, table_shape, 0)
    source = lax.broadcasted_iota(jnp.int32, table_shape, 1) + first_source
    target = lax.broadcasted_iota(jnp.int32, table_shape, 2)
    matches = source - target == offset_level
    return matches.astype(jnp.bfloat16)


def band_of(stencil, col_count, first_source=0, source_count=None):
    return jnp.einsum(
        "kiad,dpq->iapkq",
        stencil,
        lon_picker(col_count, first_source, source_count),
        preferred_element_type=jnp.float32,
    ).astype(jnp.bfloat16)


def spread(values, band, basis_count):
    row_count = values.shape[1] - 2 * LAT_REACH
    lat_taps = 2 * LAT_REACH + 1
    stacked = jnp.stack(
        [values[:, offset : offset + row_count] for offset in range(lat_taps)], axis=2
    )
    return jnp.einsum("ciap,iapkq->cikq", stacked, band, preferred_element_type=jnp.float32)


def spread_adjoint(mixed, band):
    row_count, col_count = mixed.shape[1], mixed.shape[3]
    lat_taps = 2 * LAT_REACH + 1
    partial = jnp.einsum("cikq,iapkq->ciap", mixed, band, preferred_element_type=jnp.float32)
    if partial.shape[3] != col_count - LON_HALO:
        partial = partial[:, :, :, LON_HALO : col_count]
    out_rows = row_count - LAT_HALO
    total = partial[:, LAT_HALO : LAT_HALO + out_rows, 0]
    for offset in range(1, lat_taps):
        start = LAT_HALO - offset
        total = total + partial[:, start : start + out_rows, offset]
    return total


def spread_adjoint_rows(mixed, band):
    col_count = mixed.shape[3]
    partial = jnp.einsum("cikq,iapkq->ciap", mixed, band, preferred_element_type=jnp.float32)
    if partial.shape[3] != col_count - LON_HALO:
        partial = partial[:, :, :, LON_HALO : col_count]
    below = jnp.pad(partial[:, 1:, 0], ((0, 0), (0, 1), (0, 0)))
    above = jnp.pad(partial[:, :-1, 2], ((0, 0), (1, 0), (0, 0)))
    return partial[:, :, 1] + below + above


def mix_channels(weight, spreaded):
    return jnp.einsum("koc,cikj->oij", weight, spreaded, preferred_element_type=jnp.float32)


def unmix(weight, grad_rows):
    return jnp.einsum(
        "koc,oij->cikj", weight, grad_rows, preferred_element_type=jnp.float32
    ).astype(jnp.bfloat16)


def filter_term(gradient, spreaded):
    return jnp.einsum("oij,cikj->koc", gradient, spreaded, preferred_element_type=jnp.float32)


def body(state_field, first_weight, second_weight, quadrature, lat_offsets, lon_offsets, cotangent):
    source = state_field[0]
    gradient = cotangent[0]
    channels, row_count, col_count = source.shape
    stencil = coefficients(quadrature, lat_offsets, lon_offsets)
    basis_count = stencil.shape[0]

    packed = lon_halo(jnp.concatenate([source, gradient], axis=0), LON_HALO)
    taps_per_row = stencil.size // row_count
    stencil_rows = jnp.transpose(stencil, (1, 0, 2, 3)).reshape(row_count, taps_per_row)
    stencil_rows = jnp.pad(stencil_rows, ((0, 0), (0, packed.shape[2] - taps_per_row)))
    framed = lat_halo(jnp.concatenate([packed, stencil_rows[None]], axis=0), 1, LAT_HALO)
    source_wide, gradient_wide = framed[:channels], framed[channels : 2 * channels]
    stencil_wide = framed[2 * channels, :, :taps_per_row].reshape(
        row_count + 2 * LAT_HALO, stencil.shape[0], stencil.shape[2], stencil.shape[3]
    )
    stencil_wide = jnp.transpose(stencil_wide, (1, 0, 2, 3))

    total_rows = row_count * lax.axis_size("lat")
    first_row = lax.axis_index("lat") * row_count
    near_rows = first_row - LAT_REACH + jnp.arange(row_count + 2 * LAT_REACH)
    near_valid = ((near_rows >= 0) & (near_rows < total_rows))[None, :, None]

    near_band = band_of(stencil_wide[:, LAT_REACH : LAT_REACH + row_count + 2 * LAT_REACH], col_count + LON_HALO)
    own_band = band_of(stencil, col_count)
    wide_band = band_of(stencil_wide, col_count + 2 * LON_HALO, LON_HALO, col_count + LON_HALO)

    first_near = spread(source_wide, near_band, basis_count).astype(jnp.bfloat16)
    hidden = mix_channels(first_weight, first_near)
    activation = jnp.where(near_valid, jax.nn.gelu(hidden), 0.0).astype(jnp.bfloat16)
    second_spread = spread(activation, own_band, basis_count).astype(jnp.bfloat16)
    own_gradient = gradient_wide[:, LAT_HALO : LAT_HALO + row_count, LON_HALO : LON_HALO + col_count]
    second_sum = filter_term(own_gradient, second_spread)

    if lax.axis_size("lat") == 2 and row_count == LAT_HALO:
        lower = lax.axis_index("lat") == 0
        grid_gradient = jnp.where(lower, gradient_wide[:, row_count:], gradient_wide[:, : 2 * row_count])
        grid_stencil = jnp.where(lower, stencil_wide[:, row_count:], stencil_wide[:, : 2 * row_count])
        grid_band = band_of(grid_stencil, col_count + 2 * LON_HALO, LON_HALO, col_count + LON_HALO)
        second_mixed = unmix(second_weight, grid_gradient)
        grid_grad = spread_adjoint_rows(second_mixed, grid_band).astype(jnp.bfloat16)
        edge = jnp.zeros_like(grid_grad[:, :LAT_REACH])
        activation_grad = jnp.where(
            lower,
            jnp.concatenate([edge, grid_grad[:, : 2 * row_count - LAT_REACH]], axis=1),
            jnp.concatenate([grid_grad[:, LAT_REACH:], edge], axis=1),
        )
    else:
        second_mixed = unmix(second_weight, gradient_wide)
        activation_grad = spread_adjoint(second_mixed, wide_band).astype(jnp.bfloat16)
    hidden_grad = jax.vjp(jax.nn.gelu, hidden)[1](activation_grad.astype(jnp.float32))[0]
    hidden_grad = jnp.where(near_valid, hidden_grad, 0.0).astype(jnp.bfloat16)
    own_hidden_grad = hidden_grad[:, LAT_REACH : LAT_REACH + row_count, LON_REACH : LON_REACH + col_count]
    own_first = first_near[:, LAT_REACH : LAT_REACH + row_count, :, LON_REACH : LON_REACH + col_count]
    first_sum = filter_term(own_hidden_grad, own_first)
    member_total = state_field.shape[0] * lax.axis_size("ens")
    grad_scale = 1.0 / math.sqrt(
        member_total * row_count * lax.axis_size("lat") * col_count * lax.axis_size("lon")
    )
    axes = ("ens", "lat", "lon")
    second_grad, second_spread = halving_sum(second_sum * grad_scale, axes, hold=second_spread)
    first_grad, hidden_grad = halving_sum(first_sum * grad_scale, axes, hold=hidden_grad)
    layer_output = mix_channels(second_weight, second_spread).astype(jnp.bfloat16)
    first_mixed = unmix(first_weight, hidden_grad)
    state_grad = spread_adjoint(first_mixed, near_band).astype(jnp.bfloat16)
    return (layer_output[None], state_grad[None], first_grad, second_grad)


def solution(mesh):
    in_specs = (
        P("ens", None, "lat", "lon"),
        P(),
        P(),
        P("lat", None, None),
        P("lat", None, None),
        P("lat", None, None),
        P("ens", None, "lat", "lon"),
    )
    out_specs = (P("ens", None, "lat", "lon"), P("ens", None, "lat", "lon"), P(), P())
    return jax.shard_map(body, mesh=mesh, in_specs=in_specs, out_specs=out_specs, check_vma=False)
```

```python
import math

import jax
import jax.numpy as jnp
from jax import lax
from jax.sharding import PartitionSpec as P

LAT_REACH = 1
LON_REACH = 4
LAT_HALO = 2 * LAT_REACH
LON_HALO = 2 * LON_REACH


def halving_sum(value, axes, exchanged=2, hold=None):
    stages = []
    for axis in axes:
        bit = 1
        while bit < lax.axis_size(axis):
            stages.append((axis, bit))
            bit *= 2
    exchanged = min(exchanged, len(stages))
    halved = stages[: len(stages) - exchanged]
    flat = value.reshape(-1, value.shape[-1])
    held = hold
    for axis, bit in halved:
        pairs = [(i, i ^ bit) for i in range(lax.axis_size(axis))]
        upper = (lax.axis_index(axis) // bit) % 2
        half = flat.shape[0] // 2
        keep = lax.dynamic_slice_in_dim(flat, upper * half, half)
        send = lax.dynamic_slice_in_dim(flat, (1 - upper) * half, half)
        flat = keep + lax.ppermute(send, axis, pairs)
        if hold is not None:
            flat, hold = lax.optimization_barrier((flat, hold))
            held, hold = hold, None
    for axis, bit in stages[len(halved) :]:
        pairs = [(i, i ^ bit) for i in range(lax.axis_size(axis))]
        flat = flat + lax.ppermute(flat, axis, pairs)
    flat = flat.astype(jnp.bfloat16)
    for step, (axis, bit) in enumerate(reversed(halved)):
        pairs = [(i, i ^ bit) for i in range(lax.axis_size(axis))]
        upper = (lax.axis_index(axis) // bit) % 2
        other = lax.ppermute(flat, axis, pairs)
        if step == len(halved) - 1:
            flat, other = flat.astype(jnp.float32), other.astype(jnp.float32)
        flat = jnp.where(
            upper == 1, jnp.concatenate([other, flat]), jnp.concatenate([flat, other])
        )
    return flat.astype(jnp.float32).reshape(value.shape), held


def lat_halo(block, dim, width):
    count = lax.axis_size("lat")
    rows = block.shape[dim]
    if count == 2 and width == rows:
        other = lax.ppermute(block, "lat", [(0, 1), (1, 0)])
        lower = lax.axis_index("lat") == 0
        blank = jnp.zeros_like(other)
        above = jnp.where(lower, blank, other)
        below = jnp.where(lower, other, blank)
        return jnp.concatenate([above, block, below], axis=dim)
    above = lax.ppermute(
        lax.slice_in_dim(block, rows - width, rows, axis=dim),
        "lat",
        [(i, i + 1) for i in range(count - 1)],
    )
    below = lax.ppermute(
        lax.slice_in_dim(block, 0, width, axis=dim), "lat", [(i + 1, i) for i in range(count - 1)]
    )
    return jnp.concatenate([above, block, below], axis=dim)


def lon_halo(block, width):
    count = lax.axis_size("lon")
    cols = block.shape[-1]
    left = lax.ppermute(block[..., cols - width :], "lon", [(i, (i + 1) % count) for i in range(count)])
    right = lax.ppermute(block[..., :width], "lon", [(i, (i - 1) % count) for i in range(count)])
    return jnp.concatenate([left, block, right], axis=-1)


def coefficients(quadrature, lat_offsets, lon_offsets):
    lat_levels = jnp.arange(2 * LAT_REACH + 1, dtype=jnp.int32)
    lon_levels = jnp.arange(2 * LON_REACH + 1, dtype=jnp.int32)
    lat_onehot = (lat_offsets[..., None] + LAT_REACH == lat_levels).astype(jnp.float32)
    lon_onehot = (lon_offsets[..., None] + LON_REACH == lon_levels).astype(jnp.float32)
    stencil = jnp.einsum(
        "rks,rksa,rksd->krad", quadrature, lat_onehot, lon_onehot, precision=lax.Precision.HIGHEST
    )
    return stencil.astype(jnp.bfloat16)


def lon_picker(col_count, first_source=0, source_count=None):
    span_count = 2 * LON_REACH + 1
    if source_count is None:
        source_count = col_count + 2 * LON_REACH
    table_shape = (span_count, source_count, col_count)
    offset_level = lax.broadcasted_iota(jnp.int32, table_shape, 0)
    source = lax.broadcasted_iota(jnp.int32, table_shape, 1) + first_source
    target = lax.broadcasted_iota(jnp.int32, table_shape, 2)
    matches = source - target == offset_level
    return matches.astype(jnp.bfloat16)


def band_of(stencil, col_count, first_source=0, source_count=None):
    return jnp.einsum(
        "kiad,dpq->iapkq",
        stencil,
        lon_picker(col_count, first_source, source_count),
        preferred_element_type=jnp.float32,
    ).astype(jnp.bfloat16)


def spread(values, band, basis_count):
    row_count = values.shape[1] - 2 * LAT_REACH
    lat_taps = 2 * LAT_REACH + 1
    stacked = jnp.stack(
        [values[:, offset : offset + row_count] for offset in range(lat_taps)], axis=2
    )
    return jnp.einsum("ciap,iapkq->cikq", stacked, band, preferred_element_type=jnp.float32)


def spread_adjoint(mixed, band):
    row_count, col_count = mixed.shape[1], mixed.shape[3]
    lat_taps = 2 * LAT_REACH + 1
    partial = jnp.einsum("cikq,iapkq->ciap", mixed, band, preferred_element_type=jnp.float32)
    if partial.shape[3] != col_count - LON_HALO:
        partial = partial[:, :, :, LON_HALO : col_count]
    out_rows = row_count - LAT_HALO
    total = partial[:, LAT_HALO : LAT_HALO + out_rows, 0]
    for offset in range(1, lat_taps):
        start = LAT_HALO - offset
        total = total + partial[:, start : start + out_rows, offset]
    return total


def spread_adjoint_rows(mixed, band):
    col_count = mixed.shape[3]
    partial = jnp.einsum("cikq,iapkq->ciap", mixed, band, preferred_element_type=jnp.float32)
    if partial.shape[3] != col_count - LON_HALO:
        partial = partial[:, :, :, LON_HALO : col_count]
    below = jnp.pad(partial[:, 1:, 0], ((0, 0), (0, 1), (0, 0)))
    above = jnp.pad(partial[:, :-1, 2], ((0, 0), (1, 0), (0, 0)))
    return partial[:, :, 1] + below + above


def mix_channels(weight, spreaded):
    return jnp.einsum("koc,cikj->oij", weight, spreaded, preferred_element_type=jnp.float32)


def unmix(weight, grad_rows):
    return jnp.einsum(
        "koc,oij->cikj", weight, grad_rows, preferred_element_type=jnp.float32
    ).astype(jnp.bfloat16)


def filter_term(gradient, spreaded):
    return jnp.einsum("oij,cikj->koc", gradient, spreaded, preferred_element_type=jnp.float32)


def body(state_field, first_weight, second_weight, quadrature, lat_offsets, lon_offsets, cotangent):
    source = state_field[0]
    gradient = cotangent[0]
    channels, row_count, col_count = source.shape
    stencil = coefficients(quadrature, lat_offsets, lon_offsets)
    basis_count = stencil.shape[0]

    packed = lon_halo(jnp.concatenate([source, gradient], axis=0), LON_HALO)
    taps_per_row = stencil.size // row_count
    stencil_rows = jnp.transpose(stencil, (1, 0, 2, 3)).reshape(row_count, taps_per_row)
    stencil_rows = jnp.pad(stencil_rows, ((0, 0), (0, packed.shape[2] - taps_per_row)))
    framed = lat_halo(jnp.concatenate([packed, stencil_rows[None]], axis=0), 1, LAT_HALO)
    source_wide, gradient_wide = framed[:channels], framed[channels : 2 * channels]
    stencil_wide = framed[2 * channels, :, :taps_per_row].reshape(
        row_count + 2 * LAT_HALO, stencil.shape[0], stencil.shape[2], stencil.shape[3]
    )
    stencil_wide = jnp.transpose(stencil_wide, (1, 0, 2, 3))

    total_rows = row_count * lax.axis_size("lat")
    first_row = lax.axis_index("lat") * row_count
    near_rows = first_row - LAT_REACH + jnp.arange(row_count + 2 * LAT_REACH)
    near_valid = ((near_rows >= 0) & (near_rows < total_rows))[None, :, None]

    near_band = band_of(stencil_wide[:, LAT_REACH : LAT_REACH + row_count + 2 * LAT_REACH], col_count + LON_HALO)
    own_band = band_of(stencil, col_count)
    wide_band = band_of(stencil_wide, col_count + 2 * LON_HALO, LON_HALO, col_count + LON_HALO)

    first_near = spread(source_wide, near_band, basis_count).astype(jnp.bfloat16)
    hidden = mix_channels(first_weight, first_near)
    activation = jnp.where(near_valid, jax.nn.gelu(hidden), 0.0).astype(jnp.bfloat16)
    second_spread = spread(activation, own_band, basis_count).astype(jnp.bfloat16)
    own_gradient = gradient_wide[:, LAT_HALO : LAT_HALO + row_count, LON_HALO : LON_HALO + col_count]
    second_sum = filter_term(own_gradient, second_spread)

    member_total = state_field.shape[0] * lax.axis_size("ens")
    grad_scale = 1.0 / math.sqrt(
        member_total * row_count * lax.axis_size("lat") * col_count * lax.axis_size("lon")
    )
    axes = ("ens", "lat", "lon")
    second_grad, (second_spread, gradient_wide) = halving_sum(
        second_sum * grad_scale, axes, hold=(second_spread, gradient_wide)
    )

    if lax.axis_size("lat") == 2 and row_count == LAT_HALO:
        lower = lax.axis_index("lat") == 0
        grid_gradient = jnp.where(lower, gradient_wide[:, row_count:], gradient_wide[:, : 2 * row_count])
        grid_stencil = jnp.where(lower, stencil_wide[:, row_count:], stencil_wide[:, : 2 * row_count])
        grid_band = band_of(grid_stencil, col_count + 2 * LON_HALO, LON_HALO, col_count + LON_HALO)
        second_mixed = unmix(second_weight, grid_gradient)
        grid_grad = spread_adjoint_rows(second_mixed, grid_band).astype(jnp.bfloat16)
        edge = jnp.zeros_like(grid_grad[:, :LAT_REACH])
        activation_grad = jnp.where(
            lower,
            jnp.concatenate([edge, grid_grad[:, : 2 * row_count - LAT_REACH]], axis=1),
            jnp.concatenate([grid_grad[:, LAT_REACH:], edge], axis=1),
        )
    else:
        second_mixed = unmix(second_weight, gradient_wide)
        activation_grad = spread_adjoint(second_mixed, wide_band).astype(jnp.bfloat16)
    hidden_grad = jax.vjp(jax.nn.gelu, hidden)[1](activation_grad.astype(jnp.float32))[0]
    hidden_grad = jnp.where(near_valid, hidden_grad, 0.0).astype(jnp.bfloat16)
    own_hidden_grad = hidden_grad[:, LAT_REACH : LAT_REACH + row_count, LON_REACH : LON_REACH + col_count]
    own_first = first_near[:, LAT_REACH : LAT_REACH + row_count, :, LON_REACH : LON_REACH + col_count]
    first_sum = filter_term(own_hidden_grad, own_first)
    first_grad, hidden_grad = halving_sum(first_sum * grad_scale, axes, hold=hidden_grad)
    layer_output = mix_channels(second_weight, second_spread).astype(jnp.bfloat16)
    first_mixed = unmix(first_weight, hidden_grad)
    state_grad = spread_adjoint(first_mixed, near_band).astype(jnp.bfloat16)
    return (layer_output[None], state_grad[None], first_grad, second_grad)


def solution(mesh):
    in_specs = (
        P("ens", None, "lat", "lon"),
        P(),
        P(),
        P("lat", None, None),
        P("lat", None, None),
        P("lat", None, None),
        P("ens", None, "lat", "lon"),
    )
    out_specs = (P("ens", None, "lat", "lon"), P("ens", None, "lat", "lon"), P(), P())
    return jax.shard_map(body, mesh=mesh, in_specs=in_specs, out_specs=out_specs, check_vma=False)
```

```python
import math

import jax
import jax.numpy as jnp
from jax import lax
from jax.sharding import PartitionSpec as P

LAT_REACH = 1
LON_REACH = 4
LAT_HALO = 2 * LAT_REACH
LON_HALO = 2 * LON_REACH


def halving_sum(value, axes, exchanged=2, hold=None, late=None):
    stages = []
    for axis in axes:
        bit = 1
        while bit < lax.axis_size(axis):
            stages.append((axis, bit))
            bit *= 2
    exchanged = min(exchanged, len(stages))
    halved = stages[: len(stages) - exchanged]
    flat = value.reshape(-1, value.shape[-1])
    held = hold
    for axis, bit in halved:
        pairs = [(i, i ^ bit) for i in range(lax.axis_size(axis))]
        upper = (lax.axis_index(axis) // bit) % 2
        half = flat.shape[0] // 2
        keep = lax.dynamic_slice_in_dim(flat, upper * half, half)
        send = lax.dynamic_slice_in_dim(flat, (1 - upper) * half, half)
        flat = keep + lax.ppermute(send, axis, pairs)
        if hold is not None:
            flat, hold = lax.optimization_barrier((flat, hold))
            held, hold = hold, None
            if late is not None:
                held = late(held)
    for axis, bit in stages[len(halved) :]:
        pairs = [(i, i ^ bit) for i in range(lax.axis_size(axis))]
        flat = flat + lax.ppermute(flat, axis, pairs)
    if late is not None:
        flat, held = lax.optimization_barrier((flat, held))
    flat = flat.astype(jnp.bfloat16)
    for step, (axis, bit) in enumerate(reversed(halved)):
        pairs = [(i, i ^ bit) for i in range(lax.axis_size(axis))]
        upper = (lax.axis_index(axis) // bit) % 2
        other = lax.ppermute(flat, axis, pairs)
        if step == len(halved) - 1:
            flat, other = flat.astype(jnp.float32), other.astype(jnp.float32)
        flat = jnp.where(
            upper == 1, jnp.concatenate([other, flat]), jnp.concatenate([flat, other])
        )
    return flat.astype(jnp.float32).reshape(value.shape), held


def lat_halo(block, dim, width):
    count = lax.axis_size("lat")
    rows = block.shape[dim]
    if count == 2 and width == rows:
        other = lax.ppermute(block, "lat", [(0, 1), (1, 0)])
        lower = lax.axis_index("lat") == 0
        blank = jnp.zeros_like(other)
        above = jnp.where(lower, blank, other)
        below = jnp.where(lower, other, blank)
        return jnp.concatenate([above, block, below], axis=dim)
    above = lax.ppermute(
        lax.slice_in_dim(block, rows - width, rows, axis=dim),
        "lat",
        [(i, i + 1) for i in range(count - 1)],
    )
    below = lax.ppermute(
        lax.slice_in_dim(block, 0, width, axis=dim), "lat", [(i + 1, i) for i in range(count - 1)]
    )
    return jnp.concatenate([above, block, below], axis=dim)


def lon_halo(block, width):
    count = lax.axis_size("lon")
    cols = block.shape[-1]
    left = lax.ppermute(block[..., cols - width :], "lon", [(i, (i + 1) % count) for i in range(count)])
    right = lax.ppermute(block[..., :width], "lon", [(i, (i - 1) % count) for i in range(count)])
    return jnp.concatenate([left, block, right], axis=-1)


def coefficients(quadrature, lat_offsets, lon_offsets):
    lat_levels = jnp.arange(2 * LAT_REACH + 1, dtype=jnp.int32)
    lon_levels = jnp.arange(2 * LON_REACH + 1, dtype=jnp.int32)
    lat_onehot = (lat_offsets[..., None] + LAT_REACH == lat_levels).astype(jnp.float32)
    lon_onehot = (lon_offsets[..., None] + LON_REACH == lon_levels).astype(jnp.float32)
    stencil = jnp.einsum(
        "rks,rksa,rksd->krad", quadrature, lat_onehot, lon_onehot, precision=lax.Precision.HIGHEST
    )
    return stencil.astype(jnp.bfloat16)


def lon_picker(col_count, first_source=0, source_count=None):
    span_count = 2 * LON_REACH + 1
    if source_count is None:
        source_count = col_count + 2 * LON_REACH
    table_shape = (span_count, source_count, col_count)
    offset_level = lax.broadcasted_iota(jnp.int32, table_shape, 0)
    source = lax.broadcasted_iota(jnp.int32, table_shape, 1) + first_source
    target = lax.broadcasted_iota(jnp.int32, table_shape, 2)
    matches = source - target == offset_level
    return matches.astype(jnp.bfloat16)


def band_of(stencil, col_count, first_source=0, source_count=None):
    return jnp.einsum(
        "kiad,dpq->iapkq",
        stencil,
        lon_picker(col_count, first_source, source_count),
        preferred_element_type=jnp.float32,
    ).astype(jnp.bfloat16)


def spread(values, band, basis_count):
    row_count = values.shape[1] - 2 * LAT_REACH
    lat_taps = 2 * LAT_REACH + 1
    stacked = jnp.stack(
        [values[:, offset : offset + row_count] for offset in range(lat_taps)], axis=2
    )
    return jnp.einsum("ciap,iapkq->cikq", stacked, band, preferred_element_type=jnp.float32)


def spread_adjoint(mixed, band):
    row_count, col_count = mixed.shape[1], mixed.shape[3]
    lat_taps = 2 * LAT_REACH + 1
    partial = jnp.einsum("cikq,iapkq->ciap", mixed, band, preferred_element_type=jnp.float32)
    if partial.shape[3] != col_count - LON_HALO:
        partial = partial[:, :, :, LON_HALO : col_count]
    out_rows = row_count - LAT_HALO
    total = partial[:, LAT_HALO : LAT_HALO + out_rows, 0]
    for offset in range(1, lat_taps):
        start = LAT_HALO - offset
        total = total + partial[:, start : start + out_rows, offset]
    return total


def spread_adjoint_rows(mixed, band):
    col_count = mixed.shape[3]
    partial = jnp.einsum("cikq,iapkq->ciap", mixed, band, preferred_element_type=jnp.float32)
    if partial.shape[3] != col_count - LON_HALO:
        partial = partial[:, :, :, LON_HALO : col_count]
    below = jnp.pad(partial[:, 1:, 0], ((0, 0), (0, 1), (0, 0)))
    above = jnp.pad(partial[:, :-1, 2], ((0, 0), (1, 0), (0, 0)))
    return partial[:, :, 1] + below + above


def mix_channels(weight, spreaded):
    return jnp.einsum("koc,cikj->oij", weight, spreaded, preferred_element_type=jnp.float32)


def unmix(weight, grad_rows):
    return jnp.einsum(
        "koc,oij->cikj", weight, grad_rows, preferred_element_type=jnp.float32
    ).astype(jnp.bfloat16)


def filter_term(gradient, spreaded):
    return jnp.einsum("oij,cikj->koc", gradient, spreaded, preferred_element_type=jnp.float32)


def body(state_field, first_weight, second_weight, quadrature, lat_offsets, lon_offsets, cotangent):
    source = state_field[0]
    gradient = cotangent[0]
    channels, row_count, col_count = source.shape
    stencil = coefficients(quadrature, lat_offsets, lon_offsets)
    basis_count = stencil.shape[0]

    packed = lon_halo(jnp.concatenate([source, gradient], axis=0), LON_HALO)
    taps_per_row = stencil.size // row_count
    stencil_rows = jnp.transpose(stencil, (1, 0, 2, 3)).reshape(row_count, taps_per_row)
    stencil_rows = jnp.pad(stencil_rows, ((0, 0), (0, packed.shape[2] - taps_per_row)))
    framed = lat_halo(jnp.concatenate([packed, stencil_rows[None]], axis=0), 1, LAT_HALO)
    source_wide, gradient_wide = framed[:channels], framed[channels : 2 * channels]
    stencil_wide = framed[2 * channels, :, :taps_per_row].reshape(
        row_count + 2 * LAT_HALO, stencil.shape[0], stencil.shape[2], stencil.shape[3]
    )
    stencil_wide = jnp.transpose(stencil_wide, (1, 0, 2, 3))

    total_rows = row_count * lax.axis_size("lat")
    first_row = lax.axis_index("lat") * row_count
    near_rows = first_row - LAT_REACH + jnp.arange(row_count + 2 * LAT_REACH)
    near_valid = ((near_rows >= 0) & (near_rows < total_rows))[None, :, None]

    near_band = band_of(stencil_wide[:, LAT_REACH : LAT_REACH + row_count + 2 * LAT_REACH], col_count + LON_HALO)
    own_band = band_of(stencil, col_count)
    wide_band = band_of(stencil_wide, col_count + 2 * LON_HALO, LON_HALO, col_count + LON_HALO)

    first_near = spread(source_wide, near_band, basis_count).astype(jnp.bfloat16)
    hidden = mix_channels(first_weight, first_near)
    activation = jnp.where(near_valid, jax.nn.gelu(hidden), 0.0).astype(jnp.bfloat16)
    second_spread = spread(activation, own_band, basis_count).astype(jnp.bfloat16)
    own_gradient = gradient_wide[:, LAT_HALO : LAT_HALO + row_count, LON_HALO : LON_HALO + col_count]
    second_sum = filter_term(own_gradient, second_spread)

    if lax.axis_size("lat") == 2 and row_count == LAT_HALO:
        lower = lax.axis_index("lat") == 0
        grid_gradient = jnp.where(lower, gradient_wide[:, row_count:], gradient_wide[:, : 2 * row_count])
        grid_stencil = jnp.where(lower, stencil_wide[:, row_count:], stencil_wide[:, : 2 * row_count])
        grid_band = band_of(grid_stencil, col_count + 2 * LON_HALO, LON_HALO, col_count + LON_HALO)
        second_mixed = unmix(second_weight, grid_gradient)
        grid_grad = spread_adjoint_rows(second_mixed, grid_band).astype(jnp.bfloat16)
        edge = jnp.zeros_like(grid_grad[:, :LAT_REACH])
        activation_grad = jnp.where(
            lower,
            jnp.concatenate([edge, grid_grad[:, : 2 * row_count - LAT_REACH]], axis=1),
            jnp.concatenate([grid_grad[:, LAT_REACH:], edge], axis=1),
        )
    else:
        second_mixed = unmix(second_weight, gradient_wide)
        activation_grad = spread_adjoint(second_mixed, wide_band).astype(jnp.bfloat16)
    hidden_grad = jax.vjp(jax.nn.gelu, hidden)[1](activation_grad.astype(jnp.float32))[0]
    hidden_grad = jnp.where(near_valid, hidden_grad, 0.0).astype(jnp.bfloat16)
    own_hidden_grad = hidden_grad[:, LAT_REACH : LAT_REACH + row_count, LON_REACH : LON_REACH + col_count]
    own_first = first_near[:, LAT_REACH : LAT_REACH + row_count, :, LON_REACH : LON_REACH + col_count]
    first_sum = filter_term(own_hidden_grad, own_first)
    member_total = state_field.shape[0] * lax.axis_size("ens")
    grad_scale = 1.0 / math.sqrt(
        member_total * row_count * lax.axis_size("lat") * col_count * lax.axis_size("lon")
    )
    axes = ("ens", "lat", "lon")

    def layer_output_of(spreaded):
        return mix_channels(second_weight, spreaded).astype(jnp.bfloat16)[None]

    def state_grad_of(grad_rows):
        first_mixed = unmix(first_weight, grad_rows)
        return spread_adjoint(first_mixed, near_band).astype(jnp.bfloat16)[None]

    second_grad, layer_output = halving_sum(
        second_sum * grad_scale, axes, hold=second_spread, late=layer_output_of
    )
    first_grad, state_grad = halving_sum(
        first_sum * grad_scale, axes, hold=hidden_grad, late=state_grad_of
    )
    return (layer_output, state_grad, first_grad, second_grad)


def solution(mesh):
    in_specs = (
        P("ens", None, "lat", "lon"),
        P(),
        P(),
        P("lat", None, None),
        P("lat", None, None),
        P("lat", None, None),
        P("ens", None, "lat", "lon"),
    )
    out_specs = (P("ens", None, "lat", "lon"), P("ens", None, "lat", "lon"), P(), P())
    return jax.shard_map(body, mesh=mesh, in_specs=in_specs, out_specs=out_specs, check_vma=False)
```

```python
import math

import jax
import jax.numpy as jnp
from jax import lax
from jax.sharding import PartitionSpec as P

LAT_REACH = 1
LON_REACH = 4
LAT_HALO = 2 * LAT_REACH
LON_HALO = 2 * LON_REACH


def halving_sum(value, axes, exchanged=2, hold=None):
    stages = []
    for axis in axes:
        bit = 1
        while bit < lax.axis_size(axis):
            stages.append((axis, bit))
            bit *= 2
    exchanged = min(exchanged, len(stages))
    halved = stages[: len(stages) - exchanged]
    flat = value.reshape(-1, value.shape[-1])
    held = hold
    for axis, bit in halved:
        pairs = [(i, i ^ bit) for i in range(lax.axis_size(axis))]
        upper = (lax.axis_index(axis) // bit) % 2
        half = flat.shape[0] // 2
        keep = lax.dynamic_slice_in_dim(flat, upper * half, half)
        send = lax.dynamic_slice_in_dim(flat, (1 - upper) * half, half)
        flat = keep + lax.ppermute(send, axis, pairs)
        if hold is not None:
            flat, hold = lax.optimization_barrier((flat, hold))
            held, hold = hold, None
    for axis, bit in stages[len(halved) :]:
        pairs = [(i, i ^ bit) for i in range(lax.axis_size(axis))]
        flat = flat + lax.ppermute(flat, axis, pairs)
    flat = flat.astype(jnp.bfloat16)
    for step, (axis, bit) in enumerate(reversed(halved)):
        pairs = [(i, i ^ bit) for i in range(lax.axis_size(axis))]
        upper = (lax.axis_index(axis) // bit) % 2
        other = lax.ppermute(flat, axis, pairs)
        if step == len(halved) - 1:
            flat, other = flat.astype(jnp.float32), other.astype(jnp.float32)
        flat = jnp.where(
            upper == 1, jnp.concatenate([other, flat]), jnp.concatenate([flat, other])
        )
    return flat.astype(jnp.float32).reshape(value.shape), held


def lat_halo(block, dim, width):
    count = lax.axis_size("lat")
    rows = block.shape[dim]
    if count == 2 and width == rows:
        other = lax.ppermute(block, "lat", [(0, 1), (1, 0)])
        lower = lax.axis_index("lat") == 0
        blank = jnp.zeros_like(other)
        above = jnp.where(lower, blank, other)
        below = jnp.where(lower, other, blank)
        return jnp.concatenate([above, block, below], axis=dim)
    above = lax.ppermute(
        lax.slice_in_dim(block, rows - width, rows, axis=dim),
        "lat",
        [(i, i + 1) for i in range(count - 1)],
    )
    below = lax.ppermute(
        lax.slice_in_dim(block, 0, width, axis=dim), "lat", [(i + 1, i) for i in range(count - 1)]
    )
    return jnp.concatenate([above, block, below], axis=dim)


def lon_halo(block, width):
    count = lax.axis_size("lon")
    cols = block.shape[-1]
    left = lax.ppermute(block[..., cols - width :], "lon", [(i, (i + 1) % count) for i in range(count)])
    right = lax.ppermute(block[..., :width], "lon", [(i, (i - 1) % count) for i in range(count)])
    return jnp.concatenate([left, block, right], axis=-1)


def coefficients(quadrature, lat_offsets, lon_offsets):
    lat_levels = jnp.arange(2 * LAT_REACH + 1, dtype=jnp.int32)
    lon_levels = jnp.arange(2 * LON_REACH + 1, dtype=jnp.int32)
    lat_onehot = (lat_offsets[..., None] + LAT_REACH == lat_levels).astype(jnp.float32)
    lon_onehot = (lon_offsets[..., None] + LON_REACH == lon_levels).astype(jnp.float32)
    stencil = jnp.einsum(
        "rks,rksa,rksd->krad", quadrature, lat_onehot, lon_onehot, precision=lax.Precision.HIGHEST
    )
    return stencil.astype(jnp.bfloat16)


def lon_picker(col_count, first_source=0, source_count=None):
    span_count = 2 * LON_REACH + 1
    if source_count is None:
        source_count = col_count + 2 * LON_REACH
    table_shape = (span_count, source_count, col_count)
    offset_level = lax.broadcasted_iota(jnp.int32, table_shape, 0)
    source = lax.broadcasted_iota(jnp.int32, table_shape, 1) + first_source
    target = lax.broadcasted_iota(jnp.int32, table_shape, 2)
    matches = source - target == offset_level
    return matches.astype(jnp.bfloat16)


def band_of(stencil, col_count, first_source=0, source_count=None):
    return jnp.einsum(
        "kiad,dpq->iapkq",
        stencil,
        lon_picker(col_count, first_source, source_count),
        preferred_element_type=jnp.float32,
    ).astype(jnp.bfloat16)


def spread(values, band, basis_count):
    row_count = values.shape[1] - 2 * LAT_REACH
    lat_taps = 2 * LAT_REACH + 1
    stacked = jnp.stack(
        [values[:, offset : offset + row_count] for offset in range(lat_taps)], axis=2
    )
    return jnp.einsum("ciap,iapkq->cikq", stacked, band, preferred_element_type=jnp.float32)


def spread_adjoint(mixed, band):
    row_count, col_count = mixed.shape[1], mixed.shape[3]
    lat_taps = 2 * LAT_REACH + 1
    partial = jnp.einsum("cikq,iapkq->ciap", mixed, band, preferred_element_type=jnp.float32)
    if partial.shape[3] != col_count - LON_HALO:
        partial = partial[:, :, :, LON_HALO : col_count]
    out_rows = row_count - LAT_HALO
    total = partial[:, LAT_HALO : LAT_HALO + out_rows, 0]
    for offset in range(1, lat_taps):
        start = LAT_HALO - offset
        total = total + partial[:, start : start + out_rows, offset]
    return total


def spread_adjoint_rows(mixed, band):
    col_count = mixed.shape[3]
    partial = jnp.einsum("cikq,iapkq->ciap", mixed, band, preferred_element_type=jnp.float32)
    if partial.shape[3] != col_count - LON_HALO:
        partial = partial[:, :, :, LON_HALO : col_count]
    below = jnp.pad(partial[:, 1:, 0], ((0, 0), (0, 1), (0, 0)))
    above = jnp.pad(partial[:, :-1, 2], ((0, 0), (1, 0), (0, 0)))
    return partial[:, :, 1] + below + above


def mix_channels(weight, spreaded):
    return jnp.einsum("koc,cikj->oij", weight, spreaded, preferred_element_type=jnp.float32)


def unmix(weight, grad_rows):
    return jnp.einsum(
        "koc,oij->cikj", weight, grad_rows, preferred_element_type=jnp.float32
    ).astype(jnp.bfloat16)


def filter_term(gradient, spreaded):
    return jnp.einsum("oij,cikj->koc", gradient, spreaded, preferred_element_type=jnp.float32)


def body(state_field, first_weight, second_weight, quadrature, lat_offsets, lon_offsets, cotangent):
    source = state_field[0]
    gradient = cotangent[0]
    channels, row_count, col_count = source.shape
    stencil = coefficients(quadrature, lat_offsets, lon_offsets)
    basis_count = stencil.shape[0]

    packed = jnp.concatenate([source, gradient], axis=0)
    taps_per_row = stencil.size // row_count
    stencil_rows = jnp.transpose(stencil, (1, 0, 2, 3)).reshape(row_count, taps_per_row)
    stencil_rows = jnp.pad(stencil_rows, ((0, 0), (0, col_count - taps_per_row)))
    tall = lat_halo(jnp.concatenate([packed, stencil_rows[None]], axis=0), 1, LAT_HALO)
    framed = lon_halo(tall[: 2 * channels], LON_HALO)
    source_wide, gradient_wide = framed[:channels], framed[channels:]
    stencil_wide = tall[2 * channels, :, :taps_per_row].reshape(
        row_count + 2 * LAT_HALO, stencil.shape[0], stencil.shape[2], stencil.shape[3]
    )
    stencil_wide = jnp.transpose(stencil_wide, (1, 0, 2, 3))

    total_rows = row_count * lax.axis_size("lat")
    first_row = lax.axis_index("lat") * row_count
    near_rows = first_row - LAT_REACH + jnp.arange(row_count + 2 * LAT_REACH)
    near_valid = ((near_rows >= 0) & (near_rows < total_rows))[None, :, None]

    near_band = band_of(stencil_wide[:, LAT_REACH : LAT_REACH + row_count + 2 * LAT_REACH], col_count + LON_HALO)
    own_band = band_of(stencil, col_count)
    wide_band = band_of(stencil_wide, col_count + 2 * LON_HALO, LON_HALO, col_count + LON_HALO)

    first_near = spread(source_wide, near_band, basis_count).astype(jnp.bfloat16)
    hidden = mix_channels(first_weight, first_near)
    activation = jnp.where(near_valid, jax.nn.gelu(hidden), 0.0).astype(jnp.bfloat16)
    second_spread = spread(activation, own_band, basis_count).astype(jnp.bfloat16)
    own_gradient = gradient_wide[:, LAT_HALO : LAT_HALO + row_count, LON_HALO : LON_HALO + col_count]
    second_sum = filter_term(own_gradient, second_spread)

    if lax.axis_size("lat") == 2 and row_count == LAT_HALO:
        lower = lax.axis_index("lat") == 0
        grid_gradient = jnp.where(lower, gradient_wide[:, row_count:], gradient_wide[:, : 2 * row_count])
        grid_stencil = jnp.where(lower, stencil_wide[:, row_count:], stencil_wide[:, : 2 * row_count])
        grid_band = band_of(grid_stencil, col_count + 2 * LON_HALO, LON_HALO, col_count + LON_HALO)
        second_mixed = unmix(second_weight, grid_gradient)
        grid_grad = spread_adjoint_rows(second_mixed, grid_band).astype(jnp.bfloat16)
        edge = jnp.zeros_like(grid_grad[:, :LAT_REACH])
        activation_grad = jnp.where(
            lower,
            jnp.concatenate([edge, grid_grad[:, : 2 * row_count - LAT_REACH]], axis=1),
            jnp.concatenate([grid_grad[:, LAT_REACH:], edge], axis=1),
        )
    else:
        second_mixed = unmix(second_weight, gradient_wide)
        activation_grad = spread_adjoint(second_mixed, wide_band).astype(jnp.bfloat16)
    hidden_grad = jax.vjp(jax.nn.gelu, hidden)[1](activation_grad.astype(jnp.float32))[0]
    hidden_grad = jnp.where(near_valid, hidden_grad, 0.0).astype(jnp.bfloat16)
    own_hidden_grad = hidden_grad[:, LAT_REACH : LAT_REACH + row_count, LON_REACH : LON_REACH + col_count]
    own_first = first_near[:, LAT_REACH : LAT_REACH + row_count, :, LON_REACH : LON_REACH + col_count]
    first_sum = filter_term(own_hidden_grad, own_first)
    member_total = state_field.shape[0] * lax.axis_size("ens")
    grad_scale = 1.0 / math.sqrt(
        member_total * row_count * lax.axis_size("lat") * col_count * lax.axis_size("lon")
    )
    axes = ("ens", "lat", "lon")
    second_grad, second_spread = halving_sum(second_sum * grad_scale, axes, hold=second_spread)
    first_grad, hidden_grad = halving_sum(first_sum * grad_scale, axes, hold=hidden_grad)
    layer_output = mix_channels(second_weight, second_spread).astype(jnp.bfloat16)
    first_mixed = unmix(first_weight, hidden_grad)
    state_grad = spread_adjoint(first_mixed, near_band).astype(jnp.bfloat16)
    return (layer_output[None], state_grad[None], first_grad, second_grad)


def solution(mesh):
    in_specs = (
        P("ens", None, "lat", "lon"),
        P(),
        P(),
        P("lat", None, None),
        P("lat", None, None),
        P("lat", None, None),
        P("ens", None, "lat", "lon"),
    )
    out_specs = (P("ens", None, "lat", "lon"), P("ens", None, "lat", "lon"), P(), P())
    return jax.shard_map(body, mesh=mesh, in_specs=in_specs, out_specs=out_specs, check_vma=False)
```

```python
import math

import jax
import jax.numpy as jnp
from jax import lax
from jax.sharding import PartitionSpec as P

LAT_REACH = 1
LON_REACH = 4
LAT_HALO = 2 * LAT_REACH
LON_HALO = 2 * LON_REACH


def halving_sum(value, axes, exchanged=2, hold=None, lead=None):
    stages = []
    for axis in axes:
        bit = 1
        while bit < lax.axis_size(axis):
            stages.append((axis, bit))
            bit *= 2
    exchanged = min(exchanged, len(stages))
    halved = stages[: len(stages) - exchanged]
    if lead is not None:
        halved = [s for s in halved if s[0] == lead] + [s for s in halved if s[0] != lead]
    flat = value.reshape(-1, value.shape[-1])
    held = hold
    for axis, bit in halved:
        pairs = [(i, i ^ bit) for i in range(lax.axis_size(axis))]
        upper = (lax.axis_index(axis) // bit) % 2
        half = flat.shape[0] // 2
        keep = lax.dynamic_slice_in_dim(flat, upper * half, half)
        send = lax.dynamic_slice_in_dim(flat, (1 - upper) * half, half)
        flat = keep + lax.ppermute(send, axis, pairs)
        if hold is not None:
            flat, hold = lax.optimization_barrier((flat, hold))
            held, hold = hold, None
    for axis, bit in stages[len(halved) :]:
        pairs = [(i, i ^ bit) for i in range(lax.axis_size(axis))]
        flat = flat + lax.ppermute(flat, axis, pairs)
    flat = flat.astype(jnp.bfloat16)
    for step, (axis, bit) in enumerate(reversed(halved)):
        pairs = [(i, i ^ bit) for i in range(lax.axis_size(axis))]
        upper = (lax.axis_index(axis) // bit) % 2
        other = lax.ppermute(flat, axis, pairs)
        if step == len(halved) - 1:
            flat, other = flat.astype(jnp.float32), other.astype(jnp.float32)
        flat = jnp.where(
            upper == 1, jnp.concatenate([other, flat]), jnp.concatenate([flat, other])
        )
    return flat.astype(jnp.float32).reshape(value.shape), held


def lat_halo(block, dim, width):
    count = lax.axis_size("lat")
    rows = block.shape[dim]
    if count == 2 and width == rows:
        other = lax.ppermute(block, "lat", [(0, 1), (1, 0)])
        lower = lax.axis_index("lat") == 0
        blank = jnp.zeros_like(other)
        above = jnp.where(lower, blank, other)
        below = jnp.where(lower, other, blank)
        return jnp.concatenate([above, block, below], axis=dim)
    above = lax.ppermute(
        lax.slice_in_dim(block, rows - width, rows, axis=dim),
        "lat",
        [(i, i + 1) for i in range(count - 1)],
    )
    below = lax.ppermute(
        lax.slice_in_dim(block, 0, width, axis=dim), "lat", [(i + 1, i) for i in range(count - 1)]
    )
    return jnp.concatenate([above, block, below], axis=dim)


def lon_halo(block, width):
    count = lax.axis_size("lon")
    cols = block.shape[-1]
    left = lax.ppermute(block[..., cols - width :], "lon", [(i, (i + 1) % count) for i in range(count)])
    right = lax.ppermute(block[..., :width], "lon", [(i, (i - 1) % count) for i in range(count)])
    return jnp.concatenate([left, block, right], axis=-1)


def coefficients(quadrature, lat_offsets, lon_offsets):
    lat_levels = jnp.arange(2 * LAT_REACH + 1, dtype=jnp.int32)
    lon_levels = jnp.arange(2 * LON_REACH + 1, dtype=jnp.int32)
    lat_onehot = (lat_offsets[..., None] + LAT_REACH == lat_levels).astype(jnp.float32)
    lon_onehot = (lon_offsets[..., None] + LON_REACH == lon_levels).astype(jnp.float32)
    stencil = jnp.einsum(
        "rks,rksa,rksd->krad", quadrature, lat_onehot, lon_onehot, precision=lax.Precision.HIGHEST
    )
    return stencil.astype(jnp.bfloat16)


def lon_picker(col_count, first_source=0, source_count=None):
    span_count = 2 * LON_REACH + 1
    if source_count is None:
        source_count = col_count + 2 * LON_REACH
    table_shape = (span_count, source_count, col_count)
    offset_level = lax.broadcasted_iota(jnp.int32, table_shape, 0)
    source = lax.broadcasted_iota(jnp.int32, table_shape, 1) + first_source
    target = lax.broadcasted_iota(jnp.int32, table_shape, 2)
    matches = source - target == offset_level
    return matches.astype(jnp.bfloat16)


def band_of(stencil, col_count, first_source=0, source_count=None):
    return jnp.einsum(
        "kiad,dpq->iapkq",
        stencil,
        lon_picker(col_count, first_source, source_count),
        preferred_element_type=jnp.float32,
    ).astype(jnp.bfloat16)


def spread(values, band, basis_count):
    row_count = values.shape[1] - 2 * LAT_REACH
    lat_taps = 2 * LAT_REACH + 1
    stacked = jnp.stack(
        [values[:, offset : offset + row_count] for offset in range(lat_taps)], axis=2
    )
    return jnp.einsum("ciap,iapkq->cikq", stacked, band, preferred_element_type=jnp.float32)


def spread_adjoint(mixed, band):
    row_count, col_count = mixed.shape[1], mixed.shape[3]
    lat_taps = 2 * LAT_REACH + 1
    partial = jnp.einsum("cikq,iapkq->ciap", mixed, band, preferred_element_type=jnp.float32)
    if partial.shape[3] != col_count - LON_HALO:
        partial = partial[:, :, :, LON_HALO : col_count]
    out_rows = row_count - LAT_HALO
    total = partial[:, LAT_HALO : LAT_HALO + out_rows, 0]
    for offset in range(1, lat_taps):
        start = LAT_HALO - offset
        total = total + partial[:, start : start + out_rows, offset]
    return total


def spread_adjoint_rows(mixed, band):
    col_count = mixed.shape[3]
    partial = jnp.einsum("cikq,iapkq->ciap", mixed, band, preferred_element_type=jnp.float32)
    if partial.shape[3] != col_count - LON_HALO:
        partial = partial[:, :, :, LON_HALO : col_count]
    below = jnp.pad(partial[:, 1:, 0], ((0, 0), (0, 1), (0, 0)))
    above = jnp.pad(partial[:, :-1, 2], ((0, 0), (1, 0), (0, 0)))
    return partial[:, :, 1] + below + above


def mix_channels(weight, spreaded):
    return jnp.einsum("koc,cikj->oij", weight, spreaded, preferred_element_type=jnp.float32)


def unmix(weight, grad_rows):
    return jnp.einsum(
        "koc,oij->cikj", weight, grad_rows, preferred_element_type=jnp.float32
    ).astype(jnp.bfloat16)


def filter_term(gradient, spreaded):
    return jnp.einsum("oij,cikj->koc", gradient, spreaded, preferred_element_type=jnp.float32)


def body(state_field, first_weight, second_weight, quadrature, lat_offsets, lon_offsets, cotangent):
    source = state_field[0]
    gradient = cotangent[0]
    channels, row_count, col_count = source.shape
    stencil = coefficients(quadrature, lat_offsets, lon_offsets)
    basis_count = stencil.shape[0]

    packed = jnp.concatenate([source, gradient], axis=0)
    taps_per_row = stencil.size // row_count
    stencil_rows = jnp.transpose(stencil, (1, 0, 2, 3)).reshape(row_count, taps_per_row)
    stencil_rows = jnp.pad(stencil_rows, ((0, 0), (0, col_count - taps_per_row)))
    tall = lat_halo(jnp.concatenate([packed, stencil_rows[None]], axis=0), 1, LAT_HALO)
    framed = lon_halo(tall[: 2 * channels], LON_HALO)
    source_wide, gradient_wide = framed[:channels], framed[channels:]
    stencil_wide = tall[2 * channels, :, :taps_per_row].reshape(
        row_count + 2 * LAT_HALO, stencil.shape[0], stencil.shape[2], stencil.shape[3]
    )
    stencil_wide = jnp.transpose(stencil_wide, (1, 0, 2, 3))

    total_rows = row_count * lax.axis_size("lat")
    first_row = lax.axis_index("lat") * row_count
    near_rows = first_row - LAT_REACH + jnp.arange(row_count + 2 * LAT_REACH)
    near_valid = ((near_rows >= 0) & (near_rows < total_rows))[None, :, None]

    near_band = band_of(stencil_wide[:, LAT_REACH : LAT_REACH + row_count + 2 * LAT_REACH], col_count + LON_HALO)
    own_band = band_of(stencil, col_count)
    wide_band = band_of(stencil_wide, col_count + 2 * LON_HALO, LON_HALO, col_count + LON_HALO)

    first_near = spread(source_wide, near_band, basis_count).astype(jnp.bfloat16)
    hidden = mix_channels(first_weight, first_near)
    activation = jnp.where(near_valid, jax.nn.gelu(hidden), 0.0).astype(jnp.bfloat16)
    second_spread = spread(activation, own_band, basis_count).astype(jnp.bfloat16)
    own_gradient = gradient_wide[:, LAT_HALO : LAT_HALO + row_count, LON_HALO : LON_HALO + col_count]
    second_sum = filter_term(own_gradient, second_spread)

    if lax.axis_size("lat") == 2 and row_count == LAT_HALO:
        lower = lax.axis_index("lat") == 0
        grid_gradient = jnp.where(lower, gradient_wide[:, row_count:], gradient_wide[:, : 2 * row_count])
        grid_stencil = jnp.where(lower, stencil_wide[:, row_count:], stencil_wide[:, : 2 * row_count])
        grid_band = band_of(grid_stencil, col_count + 2 * LON_HALO, LON_HALO, col_count + LON_HALO)
        second_mixed = unmix(second_weight, grid_gradient)
        grid_grad = spread_adjoint_rows(second_mixed, grid_band).astype(jnp.bfloat16)
        edge = jnp.zeros_like(grid_grad[:, :LAT_REACH])
        activation_grad = jnp.where(
            lower,
            jnp.concatenate([edge, grid_grad[:, : 2 * row_count - LAT_REACH]], axis=1),
            jnp.concatenate([grid_grad[:, LAT_REACH:], edge], axis=1),
        )
    else:
        second_mixed = unmix(second_weight, gradient_wide)
        activation_grad = spread_adjoint(second_mixed, wide_band).astype(jnp.bfloat16)
    hidden_grad = jax.vjp(jax.nn.gelu, hidden)[1](activation_grad.astype(jnp.float32))[0]
    hidden_grad = jnp.where(near_valid, hidden_grad, 0.0).astype(jnp.bfloat16)
    own_hidden_grad = hidden_grad[:, LAT_REACH : LAT_REACH + row_count, LON_REACH : LON_REACH + col_count]
    own_first = first_near[:, LAT_REACH : LAT_REACH + row_count, :, LON_REACH : LON_REACH + col_count]
    first_sum = filter_term(own_hidden_grad, own_first)
    member_total = state_field.shape[0] * lax.axis_size("ens")
    grad_scale = 1.0 / math.sqrt(
        member_total * row_count * lax.axis_size("lat") * col_count * lax.axis_size("lon")
    )
    axes = ("ens", "lat", "lon")
    second_grad, second_spread = halving_sum(
        second_sum * grad_scale, axes, hold=second_spread, lead="lat"
    )
    first_grad, hidden_grad = halving_sum(first_sum * grad_scale, axes, hold=hidden_grad)
    layer_output = mix_channels(second_weight, second_spread).astype(jnp.bfloat16)
    first_mixed = unmix(first_weight, hidden_grad)
    state_grad = spread_adjoint(first_mixed, near_band).astype(jnp.bfloat16)
    return (layer_output[None], state_grad[None], first_grad, second_grad)


def solution(mesh):
    in_specs = (
        P("ens", None, "lat", "lon"),
        P(),
        P(),
        P("lat", None, None),
        P("lat", None, None),
        P("lat", None, None),
        P("ens", None, "lat", "lon"),
    )
    out_specs = (P("ens", None, "lat", "lon"), P("ens", None, "lat", "lon"), P(), P())
    return jax.shard_map(body, mesh=mesh, in_specs=in_specs, out_specs=out_specs, check_vma=False)
```

```python
import math

import jax
import jax.numpy as jnp
from jax import lax
from jax.sharding import PartitionSpec as P

LAT_REACH = 1
LON_REACH = 4
LAT_HALO = 2 * LAT_REACH
LON_HALO = 2 * LON_REACH


def halving_sum(value, axes, exchanged=2, hold=None):
    stages = []
    for axis in axes:
        bit = 1
        while bit < lax.axis_size(axis):
            stages.append((axis, bit))
            bit *= 2
    exchanged = min(exchanged, len(stages))
    halved = stages[: len(stages) - exchanged]
    flat = value.reshape(-1, value.shape[-1])
    held = hold
    for axis, bit in halved:
        pairs = [(i, i ^ bit) for i in range(lax.axis_size(axis))]
        upper = (lax.axis_index(axis) // bit) % 2
        half = flat.shape[0] // 2
        keep = lax.dynamic_slice_in_dim(flat, upper * half, half)
        send = lax.dynamic_slice_in_dim(flat, (1 - upper) * half, half)
        flat = keep + lax.ppermute(send, axis, pairs)
        if hold is not None:
            flat, hold = lax.optimization_barrier((flat, hold))
            held, hold = hold, None
    for axis, bit in stages[len(halved) :]:
        pairs = [(i, i ^ bit) for i in range(lax.axis_size(axis))]
        flat = flat + lax.ppermute(flat, axis, pairs)
    flat = flat.astype(jnp.bfloat16)
    for step, (axis, bit) in enumerate(reversed(halved)):
        pairs = [(i, i ^ bit) for i in range(lax.axis_size(axis))]
        upper = (lax.axis_index(axis) // bit) % 2
        other = lax.ppermute(flat, axis, pairs)
        if step == len(halved) - 1:
            flat, other = flat.astype(jnp.float32), other.astype(jnp.float32)
        flat = jnp.where(
            upper == 1, jnp.concatenate([other, flat]), jnp.concatenate([flat, other])
        )
    return flat.astype(jnp.float32).reshape(value.shape), held


def lat_halo(block, dim, width):
    count = lax.axis_size("lat")
    rows = block.shape[dim]
    if count == 2 and width == rows:
        other = lax.ppermute(block, "lat", [(0, 1), (1, 0)])
        lower = lax.axis_index("lat") == 0
        blank = jnp.zeros_like(other)
        above = jnp.where(lower, blank, other)
        below = jnp.where(lower, other, blank)
        return jnp.concatenate([above, block, below], axis=dim)
    above = lax.ppermute(
        lax.slice_in_dim(block, rows - width, rows, axis=dim),
        "lat",
        [(i, i + 1) for i in range(count - 1)],
    )
    below = lax.ppermute(
        lax.slice_in_dim(block, 0, width, axis=dim), "lat", [(i + 1, i) for i in range(count - 1)]
    )
    return jnp.concatenate([above, block, below], axis=dim)


def lon_halo(block, width):
    count = lax.axis_size("lon")
    cols = block.shape[-1]
    left = lax.ppermute(block[..., cols - width :], "lon", [(i, (i + 1) % count) for i in range(count)])
    right = lax.ppermute(block[..., :width], "lon", [(i, (i - 1) % count) for i in range(count)])
    return jnp.concatenate([left, block, right], axis=-1)


def coefficients(quadrature, lat_offsets, lon_offsets):
    lat_levels = jnp.arange(2 * LAT_REACH + 1, dtype=jnp.int32)
    lon_levels = jnp.arange(2 * LON_REACH + 1, dtype=jnp.int32)
    lat_onehot = (lat_offsets[..., None] + LAT_REACH == lat_levels).astype(jnp.float32)
    lon_onehot = (lon_offsets[..., None] + LON_REACH == lon_levels).astype(jnp.float32)
    stencil = jnp.einsum(
        "rks,rksa,rksd->krad", quadrature, lat_onehot, lon_onehot, precision=lax.Precision.HIGHEST
    )
    return stencil.astype(jnp.bfloat16)


def lon_picker(col_count, first_source=0, source_count=None):
    span_count = 2 * LON_REACH + 1
    if source_count is None:
        source_count = col_count + 2 * LON_REACH
    table_shape = (span_count, source_count, col_count)
    offset_level = lax.broadcasted_iota(jnp.int32, table_shape, 0)
    source = lax.broadcasted_iota(jnp.int32, table_shape, 1) + first_source
    target = lax.broadcasted_iota(jnp.int32, table_shape, 2)
    matches = source - target == offset_level
    return matches.astype(jnp.bfloat16)


def band_of(stencil, col_count, first_source=0, source_count=None):
    return jnp.einsum(
        "kiad,dpq->iapkq",
        stencil,
        lon_picker(col_count, first_source, source_count),
        preferred_element_type=jnp.float32,
    ).astype(jnp.bfloat16)


def spread(values, band, basis_count):
    row_count = values.shape[1] - 2 * LAT_REACH
    lat_taps = 2 * LAT_REACH + 1
    stacked = jnp.stack(
        [values[:, offset : offset + row_count] for offset in range(lat_taps)], axis=2
    )
    return jnp.einsum("ciap,iapkq->cikq", stacked, band, preferred_element_type=jnp.float32)


def spread_adjoint(mixed, band):
    row_count, col_count = mixed.shape[1], mixed.shape[3]
    lat_taps = 2 * LAT_REACH + 1
    partial = jnp.einsum("cikq,iapkq->ciap", mixed, band, preferred_element_type=jnp.float32)
    if partial.shape[3] != col_count - LON_HALO:
        partial = partial[:, :, :, LON_HALO : col_count]
    out_rows = row_count - LAT_HALO
    total = partial[:, LAT_HALO : LAT_HALO + out_rows, 0]
    for offset in range(1, lat_taps):
        start = LAT_HALO - offset
        total = total + partial[:, start : start + out_rows, offset]
    return total


def spread_adjoint_rows(mixed, band):
    col_count = mixed.shape[3]
    partial = jnp.einsum("cikq,iapkq->ciap", mixed, band, preferred_element_type=jnp.float32)
    if partial.shape[3] != col_count - LON_HALO:
        partial = partial[:, :, :, LON_HALO : col_count]
    below = jnp.pad(partial[:, 1:, 0], ((0, 0), (0, 1), (0, 0)))
    above = jnp.pad(partial[:, :-1, 2], ((0, 0), (1, 0), (0, 0)))
    return partial[:, :, 1] + below + above


def mix_channels(weight, spreaded):
    return jnp.einsum("koc,cikj->oij", weight, spreaded, preferred_element_type=jnp.float32)


def unmix(weight, grad_rows):
    return jnp.einsum(
        "koc,oij->cikj", weight, grad_rows, preferred_element_type=jnp.float32
    ).astype(jnp.bfloat16)


def filter_term(gradient, spreaded):
    return jnp.einsum("oij,cikj->koc", gradient, spreaded, preferred_element_type=jnp.float32)


def body(state_field, first_weight, second_weight, quadrature, lat_offsets, lon_offsets, cotangent):
    source = state_field[0]
    gradient = cotangent[0]
    channels, row_count, col_count = source.shape
    stencil = coefficients(quadrature, lat_offsets, lon_offsets)
    basis_count = stencil.shape[0]

    taps_per_row = stencil.size // row_count
    stencil_rows = jnp.transpose(stencil, (1, 0, 2, 3)).reshape(row_count, taps_per_row)
    stencil_rows = jnp.pad(stencil_rows, ((0, 0), (0, col_count - taps_per_row)))
    tall = lat_halo(jnp.concatenate([source, stencil_rows[None]], axis=0), 1, LAT_HALO)
    own_rows = jnp.pad(gradient, ((0, 0), (LAT_HALO, LAT_HALO), (0, 0)))
    framed = lon_halo(jnp.concatenate([tall[:channels], own_rows], axis=0), LON_HALO)
    source_wide = framed[:channels]
    gradient_wide = lat_halo(framed[channels:, LAT_HALO : LAT_HALO + row_count], 1, LAT_HALO)
    stencil_wide = tall[channels, :, :taps_per_row].reshape(
        row_count + 2 * LAT_HALO, stencil.shape[0], stencil.shape[2], stencil.shape[3]
    )
    stencil_wide = jnp.transpose(stencil_wide, (1, 0, 2, 3))

    total_rows = row_count * lax.axis_size("lat")
    first_row = lax.axis_index("lat") * row_count
    near_rows = first_row - LAT_REACH + jnp.arange(row_count + 2 * LAT_REACH)
    near_valid = ((near_rows >= 0) & (near_rows < total_rows))[None, :, None]

    near_band = band_of(stencil_wide[:, LAT_REACH : LAT_REACH + row_count + 2 * LAT_REACH], col_count + LON_HALO)
    own_band = band_of(stencil, col_count)
    wide_band = band_of(stencil_wide, col_count + 2 * LON_HALO, LON_HALO, col_count + LON_HALO)

    first_near = spread(source_wide, near_band, basis_count).astype(jnp.bfloat16)
    hidden = mix_channels(first_weight, first_near)
    activation = jnp.where(near_valid, jax.nn.gelu(hidden), 0.0).astype(jnp.bfloat16)
    second_spread = spread(activation, own_band, basis_count).astype(jnp.bfloat16)
    own_gradient = gradient
    second_sum = filter_term(own_gradient, second_spread)

    if lax.axis_size("lat") == 2 and row_count == LAT_HALO:
        lower = lax.axis_index("lat") == 0
        grid_gradient = jnp.where(lower, gradient_wide[:, row_count:], gradient_wide[:, : 2 * row_count])
        grid_stencil = jnp.where(lower, stencil_wide[:, row_count:], stencil_wide[:, : 2 * row_count])
        grid_band = band_of(grid_stencil, col_count + 2 * LON_HALO, LON_HALO, col_count + LON_HALO)
        second_mixed = unmix(second_weight, grid_gradient)
        grid_grad = spread_adjoint_rows(second_mixed, grid_band).astype(jnp.bfloat16)
        edge = jnp.zeros_like(grid_grad[:, :LAT_REACH])
        activation_grad = jnp.where(
            lower,
            jnp.concatenate([edge, grid_grad[:, : 2 * row_count - LAT_REACH]], axis=1),
            jnp.concatenate([grid_grad[:, LAT_REACH:], edge], axis=1),
        )
    else:
        second_mixed = unmix(second_weight, gradient_wide)
        activation_grad = spread_adjoint(second_mixed, wide_band).astype(jnp.bfloat16)
    hidden_grad = jax.vjp(jax.nn.gelu, hidden)[1](activation_grad.astype(jnp.float32))[0]
    hidden_grad = jnp.where(near_valid, hidden_grad, 0.0).astype(jnp.bfloat16)
    own_hidden_grad = hidden_grad[:, LAT_REACH : LAT_REACH + row_count, LON_REACH : LON_REACH + col_count]
    own_first = first_near[:, LAT_REACH : LAT_REACH + row_count, :, LON_REACH : LON_REACH + col_count]
    first_sum = filter_term(own_hidden_grad, own_first)
    member_total = state_field.shape[0] * lax.axis_size("ens")
    grad_scale = 1.0 / math.sqrt(
        member_total * row_count * lax.axis_size("lat") * col_count * lax.axis_size("lon")
    )
    axes = ("ens", "lat", "lon")
    second_grad, second_spread = halving_sum(second_sum * grad_scale, axes, hold=second_spread)
    first_grad, hidden_grad = halving_sum(first_sum * grad_scale, axes, hold=hidden_grad)
    layer_output = mix_channels(second_weight, second_spread).astype(jnp.bfloat16)
    first_mixed = unmix(first_weight, hidden_grad)
    state_grad = spread_adjoint(first_mixed, near_band).astype(jnp.bfloat16)
    return (layer_output[None], state_grad[None], first_grad, second_grad)


def solution(mesh):
    in_specs = (
        P("ens", None, "lat", "lon"),
        P(),
        P(),
        P("lat", None, None),
        P("lat", None, None),
        P("lat", None, None),
        P("ens", None, "lat", "lon"),
    )
    out_specs = (P("ens", None, "lat", "lon"), P("ens", None, "lat", "lon"), P(), P())
    return jax.shard_map(body, mesh=mesh, in_specs=in_specs, out_specs=out_specs, check_vma=False)
```
